512 devices in a mesh: row: 4 (over z_hi), col: 16 (over z_lo, x, core), chan: 8 (over y).
Axes of the slice: x: 4, y: 8, z: 8 (z_hi: 4, z_lo: 2; z = z_hi * 2 + z_lo), core: 2. Of those that a mesh axis runs over, the one named last changes fastest.
Arguments:
- snapshots: bfloat16 [8192, 2048], P('col', 'chan'), may hold values from -45 to 45
- offsets: int32 [4], replicated, may hold values from 0 to 15
- window_len: int32 [8192], replicated, may hold values from 64 to 256, as said below
- cone_exp: int32 [8192], replicated, may hold values from 0 to 3
Outputs:
- kernel: float32 [2048, 8192], P(('row', 'chan'), 'col')
The draws below stay inside these ranges and needn't reach their ends.
Inputs may be any that keep to these rules, and one draw needn't show every extreme that they name: `window_len`: each value is a lag window length; at least one snapshot has a window of 256 lags.
All inputs are finite; a program needn't handle non-finite values.
Results may differ from the reference program's by a relative error of at most 0.0003.
Values may be sent and summed in bfloat16 or wider, within the bound.
No kernel may reach another device: no remote copies, remote signals or barrier semaphores. Data moves between devices by JAX's collectives and lax.ppermute only.
A program may use at most 64 MiB of HBM per device.

```python
import math
import jax
import jax.numpy as jnp
from jax import lax

C = 2048
LAGS = 256
BLOCK = 512
NSNAP = 8192
N_ROW = 4
N_COL = 16


def seasonal_part(key, day_index):
    total = jnp.zeros((NSNAP, C), jnp.float32)
    for harmonic in range(1, 5):
        amplitude = jnp.clip(jax.random.normal(jax.random.fold_in(key, 30 + harmonic), (C,), jnp.float32), -3.0, 3.0)
        offset = jax.random.randint(jax.random.fold_in(key, 40 + harmonic), (C,), 0, 365, dtype=jnp.int32)
        fraction = ((harmonic * day_index + offset[None, :]) % 365).astype(jnp.float32) / 365.0
        total = total + amplitude[None, :] * jnp.cos(2.0 * math.pi * fraction)
    return total * 0.7071


def varying_part(key, day_index):
    total = jnp.zeros((NSNAP, C), jnp.float32)
    for member in range(2):
        octave = jax.random.randint(jax.random.fold_in(key, 50 + member), (C,), 0, 9, dtype=jnp.int32)
        lowest = jnp.left_shift(jnp.full((C,), 8, jnp.int32), octave)
        period = lowest + jax.random.randint(jax.random.fold_in(key, 60 + member), (C,), 0, lowest, dtype=jnp.int32)
        offset = jax.random.randint(jax.random.fold_in(key, 70 + member), (C,), 0, period, dtype=jnp.int32)
        fraction = ((day_index + offset[None, :]) % period[None, :]).astype(jnp.float32) / period.astype(jnp.float32)[None, :]
        total = total + jnp.cos(2.0 * math.pi * fraction)
    return total


def draw_snapshots(key, part):
    key_phase = jax.random.fold_in(key, 11)
    key_level = jax.random.fold_in(key, 12)
    key_field = jax.random.fold_in(key, 13)
    key_cycles = jax.random.fold_in(key, 15)
    key_varying = jax.random.fold_in(key, 16)
    day_index = jnp.arange(NSNAP, dtype=jnp.int32)[:, None]
    moments = jnp.arange(NSNAP).astype(jnp.float32)
    phase = jax.random.uniform(key_phase, (), jnp.float32, 0.0, 2.0 * math.pi)
    level = jnp.clip(jax.random.normal(key_level, (NSNAP,), jnp.float32), -3.0, 3.0)
    seasonal = seasonal_part(key_cycles, day_index)
    varying = varying_part(key_varying, day_index)
    noise = jnp.clip(jax.random.normal(key_field, (NSNAP, C), jnp.float32), -6.0, 6.0)
    field = 0.6 * seasonal + 0.6 * varying + 0.5 * noise
    growth = 0.8 * jnp.sin(2.0 * math.pi * moments / BLOCK + phase) + 0.4 * level
    field = jnp.clip(field, -6.0, 6.0)
    values = jnp.exp(growth)[:, None] * field
    return values.astype(jnp.bfloat16)


def draw_window_len(key, part):
    key_values = jax.random.fold_in(key, 21)
    key_place = jax.random.fold_in(key, 22)
    values = jax.random.randint(key_values, (NSNAP,), LAGS // 4, LAGS + 1, dtype=jnp.int32)
    place = jax.random.randint(key_place, (), 0, NSNAP, dtype=jnp.int32)
    values = values.at[place].set(LAGS)
    values = values.at[(place + NSNAP // 2) % NSNAP].set(LAGS // 4)
    return values


def with_ends(result, stream_key, smallest, high):
    longest = result.shape.index(max(result.shape))
    spots = []
    for shift in (0, 1):
        where = [jax.random.randint(jax.random.fold_in(stream_key, axis), (), 0, length) for axis, length in enumerate(result.shape)]
        where[longest] = (where[longest] + shift) % result.shape[longest]
        spots.append(tuple(where))
    return result.at[spots[0]].set(smallest).at[spots[1]].set(high)


def setup_inputs(seed: int = 0) -> dict:
    key_list = jax.random.split(jax.random.key(seed), 5)
    snapshots = draw_snapshots(jax.random.fold_in(key_list[4], 71), 0)
    offsets = with_ends(jax.random.randint(key_list[1], (N_ROW,), 0, N_COL), jax.random.fold_in(key_list[1], 1), 0, N_COL - 1).astype(jnp.int32)
    window_len = draw_window_len(jax.random.fold_in(key_list[4], 71), 0)
    cone_exp = with_ends(jax.random.randint(key_list[3], (NSNAP,), 0, 4), jax.random.fold_in(key_list[3], 1), 0, 3).astype(jnp.int32)
    return dict(snapshots=snapshots, offsets=offsets, window_len=window_len, cone_exp=cone_exp)


epsilon = 1e-05

def power_int(frac, exps):
    square = frac * frac
    return jnp.where(exps == 0, jnp.ones_like(frac), jnp.where(exps == 1, frac, jnp.where(exps == 2, square, square * frac)))

def weight_table(lengths, exps):
    lag = lax.broadcasted_iota(jnp.int32, (lengths.shape[0], LAGS), 1)
    span = lengths[:, None]
    valid = lag < span
    frac = (span.astype(jnp.float32) - lag.astype(jnp.float32)) / span.astype(jnp.float32)
    cone = jnp.where(valid, power_int(frac, exps[:, None]), jnp.zeros_like(frac))
    return cone / lax.optimization_barrier(jnp.sum(cone, axis=1, keepdims=True))

def block_data(snapshots, window_len, cone_exp, block_index):
    begin = (block_index * BLOCK).astype(jnp.int32)
    index = (begin - (LAGS - 1) + jnp.arange(BLOCK + LAGS - 1, dtype=jnp.int32)) % NSNAP
    panel = jnp.take(snapshots, index.astype(jnp.int32), axis=0)
    norms = lax.optimization_barrier(jnp.sum(panel.astype(jnp.float32) ** 2, axis=1))
    lengths = lax.dynamic_slice_in_dim(window_len, begin, BLOCK)
    exps = lax.dynamic_slice_in_dim(cone_exp, begin, BLOCK)
    table = weight_table(lengths, exps)
    where_at = jnp.arange(BLOCK, dtype=jnp.int32)[:, None] + (LAGS - 1) - jnp.arange(LAGS, dtype=jnp.int32)[None, :]
    scale = jnp.sqrt(lax.optimization_barrier(jnp.sum(table * norms[where_at], axis=1)) / C + epsilon)
    return (panel, norms, table, scale)

def lag_total(table, dist):

    def step(lag, total):
        shift_by = (LAGS - 1 - lag).astype(jnp.int32)
        window = lax.dynamic_slice(dist, (shift_by, shift_by), (BLOCK, BLOCK))
        column = lax.dynamic_slice_in_dim(table, lag.astype(jnp.int32), 1, 1)
        return total + column * window
    return lax.fori_loop(0, LAGS, step, jnp.zeros((BLOCK, BLOCK), jnp.float32))

def reference(snapshots, offsets, window_len, cone_exp):

    def column_block(block_index):
        return block_data(snapshots, window_len, cone_exp, block_index)
    panels, norms, tables, scales = lax.map(column_block, jnp.arange(N_COL, dtype=jnp.int32))

    def band_row(row_index):
        chosen = offsets[row_index]
        row_panel = panels[chosen]
        row_norms = norms[chosen]
        row_table = tables[chosen]
        row_scale = scales[chosen]

        def tile(col_index):
            inner = jnp.dot(row_panel, panels[col_index].T, preferred_element_type=jnp.float32)
            dist = row_norms[:, None] + norms[col_index][None, :] - 2.0 * inner
            total = lag_total(row_table, dist)
            return jnp.exp(-total / (2.0 * C * row_scale[:, None] * scales[col_index][None, :]))
        return lax.map(tile, jnp.arange(N_COL, dtype=jnp.int32))
    tiles = lax.map(band_row, jnp.arange(N_ROW, dtype=jnp.int32))
    return tiles.transpose(0, 2, 1, 3).reshape(N_ROW * BLOCK, N_COL * BLOCK)
```

```python
import jax
import jax.numpy as jnp
from jax import lax
from jax.sharding import PartitionSpec as P

C = 2048
LAGS = 256


epsilon = 1e-05


def shifted(block, axis, distance):
    devices = range(lax.axis_size(axis))
    route = [((i - distance) % len(devices), i) for i in devices]
    return lax.ppermute(block, axis, route)


def spread(value, axis, source):
    kept = jnp.where(lax.axis_index(axis) == source, value, 0).astype(value.dtype)
    return lax.psum(kept, axis)


COL_PARTS = (2, 4, 2)


def col_route(step):
    outer, mid, inner = COL_PARTS
    route = []
    for c in range(outer * mid * inner):
        z, x, k = c // (mid * inner), (c // inner) % mid, c % inner
        z, x, k = step(z, x, k)
        route.append((c, (z % outer * mid + x % mid) * inner + k % inner))
    return route


def broadcast_col(value, source):
    outer, mid, inner = COL_PARTS
    if lax.axis_size("col") != outer * mid * inner or mid != 4 or outer != 2 or inner != 2:
        return spread(value, "col", source)
    me = lax.axis_index("col")
    dz = (me // (mid * inner) - source // (mid * inner)) % outer
    dx = ((me // inner) % mid - (source // inner) % mid) % mid
    dk = (me % inner - source % inner) % inner
    got = lax.ppermute(value, "col", col_route(lambda z, x, k: (z, x, k + 1)))
    value = jnp.where(dk == 1, got, value)
    plus = col_route(lambda z, x, k: (z, x + 1, k))
    minus = col_route(lambda z, x, k: (z, x - 1, k))
    from_left = lax.ppermute(value, "col", plus)
    from_right = lax.ppermute(value, "col", minus)
    value = jnp.where(dx == 1, from_left, jnp.where(dx == 3, from_right, value))
    half = value.shape[0] // 2
    first = lax.ppermute(value[:half], "col", plus)
    second = lax.ppermute(value[half:], "col", minus)
    value = jnp.where(dx == 2, jnp.concatenate([first, second], axis=0), value)
    got = lax.ppermute(value, "col", col_route(lambda z, x, k: (z + 1, x, k)))
    return jnp.where(dz == 1, got, value)


def power_int(frac, exps):
    square = frac * frac
    return jnp.where(
        exps == 0,
        jnp.ones_like(frac),
        jnp.where(exps == 1, frac, jnp.where(exps == 2, square, square * frac)),
    )


def cone_matrix(lengths, exps, lags):
    rows = lengths.shape[0]
    row_pos = lax.broadcasted_iota(jnp.int32, (rows, rows + lags - 1), 0)
    col_pos = lax.broadcasted_iota(jnp.int32, (rows, rows + lags - 1), 1)
    lag = row_pos + (lags - 1) - col_pos
    span = lengths[:, None]
    valid = (lag >= 0) & (lag < span)
    frac = (span.astype(jnp.float32) - lag.astype(jnp.float32)) / span.astype(jnp.float32)
    cone = jnp.where(valid, power_int(frac, exps[:, None]), jnp.zeros_like(frac))
    return cone / jnp.sum(cone, axis=1, keepdims=True)


def lag_sum(weights, dist, count):
    depth = dist.shape[0]
    width = dist.shape[1]
    columns = width - (depth - count)
    padded = jnp.pad(dist, ((0, 0), (count - 1, 0)))
    stride = width + count - 1
    flat = jnp.pad(padded.reshape(-1), (0, depth))
    skewed = flat.reshape(depth, stride + 1)[:, : columns + count - 1]
    diagonal = jnp.dot(
        weights, skewed, precision=lax.Precision.HIGHEST, preferred_element_type=jnp.float32
    )
    lined = diagonal.reshape(-1)[count - 1 : count - 1 + count * (columns + count - 2)]
    return lined.reshape(count, columns + count - 2)[:, :columns]


def shards(snapshots, offsets, window_len, cone_exp):
    block = snapshots.shape[0]
    lags = LAGS
    tail = snapshots[block - (lags - 1) :]
    history = shifted(tail, "col", 1)
    col_ext = jnp.concatenate([history, snapshots], axis=0)
    chosen = lax.dynamic_index_in_dim(offsets, lax.axis_index("row"), 0, keepdims=False)
    row_ext = broadcast_col(col_ext, chosen)
    row_begin = chosen * block
    col_begin = lax.axis_index("col") * block
    row_weights = cone_matrix(
        lax.dynamic_slice_in_dim(window_len, row_begin, block),
        lax.dynamic_slice_in_dim(cone_exp, row_begin, block),
        lags,
    )
    col_weights = cone_matrix(
        lax.dynamic_slice_in_dim(window_len, col_begin, block),
        lax.dynamic_slice_in_dim(cone_exp, col_begin, block),
        lags,
    )
    share = block // lax.axis_size("chan")
    first = lax.axis_index("chan") * share
    mine = lax.dynamic_slice(row_weights, (first, first), (share, share + lags - 1))
    row_wide = row_ext.astype(jnp.float32)
    col_wide = col_ext.astype(jnp.float32)
    row_part = jnp.sum(row_wide * row_wide, axis=1)
    col_part = jnp.sum(col_wide * col_wide, axis=1)
    inner = jnp.dot(row_ext, col_ext.T, preferred_element_type=jnp.float32)
    dist = row_part[:, None] + col_part[None, :] - 2.0 * inner
    total = lax.psum_scatter(
        lag_sum(row_weights, dist, lax.axis_size("chan") * share),
        "chan",
        scatter_dimension=0,
        tiled=True,
    )
    gathered = lax.all_gather(jnp.stack([row_part, col_part]), "chan")
    row_full, col_norms = jnp.sum(gathered, axis=0)
    row_near = lax.dynamic_slice_in_dim(row_full, first, share + lags - 1)
    row_scale = jnp.sqrt(
        jnp.dot(mine, row_near, precision=lax.Precision.HIGHEST, preferred_element_type=jnp.float32)
        / C
        + epsilon
    )
    col_scale = jnp.sqrt(
        jnp.dot(
            col_weights,
            col_norms,
            precision=lax.Precision.HIGHEST,
            preferred_element_type=jnp.float32,
        )
        / C
        + epsilon
    )
    return jnp.exp(-total / (2.0 * C * row_scale[:, None] * col_scale[None, :]))


def solution(mesh):
    in_specs = (P("col", "chan"), P(), P(), P())
    out_specs = P(("row", "chan"), "col")
    return jax.shard_map(shards, mesh=mesh, in_specs=in_specs, out_specs=out_specs, check_vma=False)
```

```python
import functools

import jax
import jax.numpy as jnp
from jax import lax
from jax.experimental import pallas as pl
from jax.experimental.pallas import tpu as pltpu
from jax.sharding import PartitionSpec as P

C = 2048
LAGS = 256


epsilon = 1e-05


def shifted(block, axis, distance):
    devices = range(lax.axis_size(axis))
    route = [((i - distance) % len(devices), i) for i in devices]
    return lax.ppermute(block, axis, route)


def spread(value, axis, source):
    kept = jnp.where(lax.axis_index(axis) == source, value, 0).astype(value.dtype)
    return lax.psum(kept, axis)


COL_PARTS = (2, 4, 2)


def col_route(step):
    outer, mid, inner = COL_PARTS
    route = []
    for c in range(outer * mid * inner):
        z, x, k = c // (mid * inner), (c // inner) % mid, c % inner
        z, x, k = step(z, x, k)
        route.append((c, (z % outer * mid + x % mid) * inner + k % inner))
    return route


def broadcast_col(value, source):
    outer, mid, inner = COL_PARTS
    if lax.axis_size("col") != outer * mid * inner or mid != 4 or outer != 2 or inner != 2:
        return spread(value, "col", source)
    me = lax.axis_index("col")
    dz = (me // (mid * inner) - source // (mid * inner)) % outer
    dx = ((me // inner) % mid - (source // inner) % mid) % mid
    dk = (me % inner - source % inner) % inner
    got = lax.ppermute(value, "col", col_route(lambda z, x, k: (z, x, k + 1)))
    value = jnp.where(dk == 1, got, value)
    plus = col_route(lambda z, x, k: (z, x + 1, k))
    minus = col_route(lambda z, x, k: (z, x - 1, k))
    from_left = lax.ppermute(value, "col", plus)
    from_right = lax.ppermute(value, "col", minus)
    value = jnp.where(dx == 1, from_left, jnp.where(dx == 3, from_right, value))
    half = value.shape[0] // 2
    first = lax.ppermute(value[:half], "col", plus)
    second = lax.ppermute(value[half:], "col", minus)
    value = jnp.where(dx == 2, jnp.concatenate([first, second], axis=0), value)
    got = lax.ppermute(value, "col", col_route(lambda z, x, k: (z + 1, x, k)))
    return jnp.where(dz == 1, got, value)


def power_int(frac, exps):
    square = frac * frac
    return jnp.where(
        exps == 0,
        jnp.ones_like(frac),
        jnp.where(exps == 1, frac, jnp.where(exps == 2, square, square * frac)),
    )


def cone_matrix(lengths, exps, lags):
    rows = lengths.shape[0]
    row_pos = lax.broadcasted_iota(jnp.int32, (rows, rows + lags - 1), 0)
    col_pos = lax.broadcasted_iota(jnp.int32, (rows, rows + lags - 1), 1)
    lag = row_pos + (lags - 1) - col_pos
    span = lengths[:, None]
    valid = (lag >= 0) & (lag < span)
    frac = (span.astype(jnp.float32) - lag.astype(jnp.float32)) / span.astype(jnp.float32)
    cone = jnp.where(valid, power_int(frac, exps[:, None]), jnp.zeros_like(frac))
    return cone / jnp.sum(cone, axis=1, keepdims=True)


def reversed_cone(lengths, exps, lags, depth):
    rows = lengths.shape[0]
    row_pos = lax.broadcasted_iota(jnp.int32, (rows, depth), 0)
    col_pos = lax.broadcasted_iota(jnp.int32, (rows, depth), 1)
    lag = row_pos + col_pos - (depth - lags)
    span = lengths[:, None]
    valid = (lag >= 0) & (lag < span)
    frac = (span.astype(jnp.float32) - lag.astype(jnp.float32)) / span.astype(jnp.float32)
    cone = jnp.where(valid, power_int(frac, exps[:, None]), jnp.zeros_like(frac))
    return cone / jnp.sum(cone, axis=1, keepdims=True)


def lag_kernel(lags, r_ref, q_ref, rp_ref, cp_ref, w_ref, o_ref):
    inner = lax.dot_general(
        r_ref[...], q_ref[...], (((1,), (1,)), ((), ())), preferred_element_type=jnp.float32
    )
    dist = rp_ref[...] + cp_ref[...] - 2.0 * inner
    width = dist.shape[1]
    depth = dist.shape[0]
    skew = pltpu.roll(dist, width - lags, 1, stride=1, stride_axis=0)
    block = o_ref.shape[1]
    chunk = 128
    band = chunk + lags
    span = block + chunk
    for m in range(o_ref.shape[0] // chunk):
        low = depth - band - chunk * m
        part = jnp.dot(
            w_ref[chunk * m : chunk * (m + 1), low : low + band],
            skew[low : low + band, low : low + span],
            precision=lax.Precision.HIGHEST,
            preferred_element_type=jnp.float32,
        )
        lined = pltpu.roll(part, span - (chunk - 1), 1, stride=1, stride_axis=0)
        o_ref[chunk * m : chunk * (m + 1), :] = lined[:, :block]


def lag_total(row_rev, col_pad, row_norm, col_norm, weights, block, lags):
    depth = row_rev.shape[0]
    width = col_pad.shape[0]
    flops = 2 * depth * width * row_rev.shape[1] + 6 * 2 * block * (128 + lags) * (block + 128)
    return pl.pallas_call(
        functools.partial(lag_kernel, lags),
        out_shape=jax.ShapeDtypeStruct((block, block), jnp.float32),
        in_specs=[pl.BlockSpec(memory_space=pltpu.VMEM)] * 5,
        out_specs=pl.BlockSpec(memory_space=pltpu.VMEM),
        cost_estimate=pl.CostEstimate(
            flops=flops, transcendentals=0, bytes_accessed=4 * (block * block + block * depth) + 2 * (depth + width) * 256
        ),
    )(row_rev, col_pad, row_norm, col_norm, weights)


def shards(snapshots, offsets, window_len, cone_exp):
    block = snapshots.shape[0]
    lags = LAGS
    tail = snapshots[block - (lags - 1) :]
    history = shifted(tail, "col", 1)
    col_ext = jnp.concatenate([history, snapshots], axis=0)
    chosen = lax.dynamic_index_in_dim(offsets, lax.axis_index("row"), 0, keepdims=False)
    row_ext = broadcast_col(col_ext, chosen)
    row_begin = chosen * block
    col_begin = lax.axis_index("col") * block
    extent = block + lags
    row_lengths = lax.dynamic_slice_in_dim(window_len, row_begin, block)
    row_exps = lax.dynamic_slice_in_dim(cone_exp, row_begin, block)
    row_weights = reversed_cone(row_lengths, row_exps, lags, extent)
    col_weights = cone_matrix(
        lax.dynamic_slice_in_dim(window_len, col_begin, block),
        lax.dynamic_slice_in_dim(cone_exp, col_begin, block),
        lags,
    )
    row_wide = row_ext.astype(jnp.float32)
    col_wide = col_ext.astype(jnp.float32)
    row_part = jnp.sum(row_wide * row_wide, axis=1)
    col_part = jnp.sum(col_wide * col_wide, axis=1)
    row_rev = jnp.pad(row_ext[::-1], ((extent - row_ext.shape[0], 0), (0, 0)))
    row_part_rev = jnp.pad(row_part[::-1], (extent - row_ext.shape[0], 0))
    width = 2 * block
    col_pad = jnp.pad(col_ext, ((0, width - col_ext.shape[0]), (0, 0)))
    col_part_pad = jnp.pad(col_part, (0, width - col_ext.shape[0]))
    total = lag_total(row_rev, col_pad, row_part_rev[:, None], col_part_pad[None, :], row_weights, block, lags)
    row_sum = jnp.dot(row_weights, row_part_rev, precision=lax.Precision.HIGHEST, preferred_element_type=jnp.float32)
    col_sum = jnp.dot(col_weights, col_part, precision=lax.Precision.HIGHEST, preferred_element_type=jnp.float32)
    n_chan = lax.axis_size("chan")
    share = block // n_chan
    tiles = total.reshape(n_chan, share, block)
    col_rows = jnp.broadcast_to(col_sum[None, None, :], (n_chan, 1, block))
    row_rows = jnp.pad(row_sum.reshape(n_chan, 1, share), ((0, 0), (0, 6), (0, block - share)))
    payload = jnp.concatenate([tiles, col_rows, row_rows], axis=1).reshape(n_chan * (share + 8), block)
    mine = lax.psum_scatter(payload, "chan", scatter_dimension=0, tiled=True)
    row_scale = jnp.sqrt(mine[share + 1, :share] / C + epsilon)
    col_scale = jnp.sqrt(mine[share] / C + epsilon)
    return jnp.exp(-mine[:share] / (2.0 * C * row_scale[:, None] * col_scale[None, :]))


def solution(mesh):
    in_specs = (P("col", "chan"), P(), P(), P())
    out_specs = P(("row", "chan"), "col")
    return jax.shard_map(shards, mesh=mesh, in_specs=in_specs, out_specs=out_specs, check_vma=False)
```

```python
import functools

import jax
import jax.numpy as jnp
from jax import lax
from jax.experimental import pallas as pl
from jax.experimental.pallas import tpu as pltpu
from jax.sharding import PartitionSpec as P

C = 2048
LAGS = 256


epsilon = 1e-05


def shifted(block, axis, distance):
    devices = range(lax.axis_size(axis))
    route = [((i - distance) % len(devices), i) for i in devices]
    return lax.ppermute(block, axis, route)


def spread(value, axis, source):
    kept = jnp.where(lax.axis_index(axis) == source, value, 0).astype(value.dtype)
    return lax.psum(kept, axis)


COL_PARTS = (2, 4, 2)


def col_route(step):
    outer, mid, inner = COL_PARTS
    route = []
    for c in range(outer * mid * inner):
        z, x, k = c // (mid * inner), (c // inner) % mid, c % inner
        z, x, k = step(z, x, k)
        route.append((c, (z % outer * mid + x % mid) * inner + k % inner))
    return route


def broadcast_band(tail, block, source):
    outer, mid, inner = COL_PARTS
    count = outer * mid * inner
    rows_total = tail.shape[0] + block.shape[0]
    if lax.axis_size("col") != count or mid != 4 or outer != 2 or inner != 2 or rows_total % 4 != 0:
        joined = jnp.concatenate([shifted(tail, "col", 1), block], axis=0)
        return spread(joined, "col", source)
    me = lax.axis_index("col")
    value = jnp.concatenate([tail, block], axis=0)
    split = tail.shape[0]
    half = rows_total // 2
    quarter = half // 2

    def deltas(origin):
        dz = (me // (mid * inner) - origin // (mid * inner)) % outer
        dx = ((me // inner) % mid - (origin // inner) % mid) % mid
        dk = (me % inner - origin % inner) % inner
        return dz, dx, dk

    tz, tx, tk = deltas((source + count - 1) % count)
    bz, bx, bk = deltas(source)
    core = me % inner
    start = core * half
    rows = start + lax.broadcasted_iota(jnp.int32, (half, 1), 0)

    def pick(tail_test, block_test):
        return jnp.where(rows < split, tail_test, block_test)

    flip = col_route(lambda z, x, k: (z, x, k + 1))
    wanted = lax.dynamic_slice_in_dim(value, (1 - core) * half, half)
    got = lax.ppermute(wanted, "col", flip)
    mine = jnp.where(pick(tk == 1, bk == 1), got, lax.dynamic_slice_in_dim(value, start, half))
    plus = col_route(lambda z, x, k: (z, x + 1, k))
    minus = col_route(lambda z, x, k: (z, x - 1, k))
    from_left = lax.ppermute(mine, "col", plus)
    from_right = lax.ppermute(mine, "col", minus)
    mine = jnp.where(pick(tx == 1, bx == 1), from_left, jnp.where(pick(tx == 3, bx == 3), from_right, mine))
    first = lax.ppermute(mine[:quarter], "col", plus)
    second = lax.ppermute(mine[quarter:], "col", minus)
    mine = jnp.where(pick(tx == 2, bx == 2), jnp.concatenate([first, second], axis=0), mine)
    got = lax.ppermute(mine, "col", col_route(lambda z, x, k: (z + 1, x, k)))
    mine = jnp.where(pick(tz == 1, bz == 1), got, mine)
    other = lax.ppermute(mine, "col", flip)
    return jnp.where(core == 0, jnp.concatenate([mine, other], axis=0), jnp.concatenate([other, mine], axis=0))


def power_int(frac, exps):
    square = frac * frac
    return jnp.where(
        exps == 0,
        jnp.ones_like(frac),
        jnp.where(exps == 1, frac, jnp.where(exps == 2, square, square * frac)),
    )


def cone_matrix(lengths, exps, lags):
    rows = lengths.shape[0]
    row_pos = lax.broadcasted_iota(jnp.int32, (rows, rows + lags - 1), 0)
    col_pos = lax.broadcasted_iota(jnp.int32, (rows, rows + lags - 1), 1)
    lag = row_pos + (lags - 1) - col_pos
    span = lengths[:, None]
    valid = (lag >= 0) & (lag < span)
    frac = (span.astype(jnp.float32) - lag.astype(jnp.float32)) / span.astype(jnp.float32)
    cone = jnp.where(valid, power_int(frac, exps[:, None]), jnp.zeros_like(frac))
    return cone / jnp.sum(cone, axis=1, keepdims=True)


def reversed_cone(lengths, exps, lags, depth):
    rows = lengths.shape[0]
    row_pos = lax.broadcasted_iota(jnp.int32, (rows, depth), 0)
    col_pos = lax.broadcasted_iota(jnp.int32, (rows, depth), 1)
    lag = row_pos + col_pos - (depth - lags)
    span = lengths[:, None]
    valid = (lag >= 0) & (lag < span)
    frac = (span.astype(jnp.float32) - lag.astype(jnp.float32)) / span.astype(jnp.float32)
    cone = jnp.where(valid, power_int(frac, exps[:, None]), jnp.zeros_like(frac))
    return cone / jnp.sum(cone, axis=1, keepdims=True)


def lag_kernel(lags, r_ref, q_ref, rp_ref, cp_ref, w_ref, o_ref):
    inner = lax.dot_general(
        r_ref[...], q_ref[...], (((1,), (1,)), ((), ())), preferred_element_type=jnp.float32
    )
    dist = rp_ref[...] + cp_ref[...] - 2.0 * inner
    width = dist.shape[1]
    depth = dist.shape[0]
    skew = pltpu.roll(dist, width - lags, 1, stride=1, stride_axis=0)
    block = o_ref.shape[1]
    chunk = 128
    band = chunk + lags
    span = block + chunk
    for m in range(o_ref.shape[0] // chunk):
        low = depth - band - chunk * m
        part = jnp.dot(
            w_ref[chunk * m : chunk * (m + 1), low : low + band],
            skew[low : low + band, low : low + span],
            precision=lax.Precision.HIGHEST,
            preferred_element_type=jnp.float32,
        )
        lined = pltpu.roll(part, span - (chunk - 1), 1, stride=1, stride_axis=0)
        o_ref[chunk * m : chunk * (m + 1), :] = lined[:, :block]


def lag_total(row_rev, col_pad, row_norm, col_norm, weights, block, lags):
    depth = row_rev.shape[0]
    width = col_pad.shape[0]
    flops = 2 * depth * width * row_rev.shape[1] + 6 * 2 * block * (128 + lags) * (block + 128)
    return pl.pallas_call(
        functools.partial(lag_kernel, lags),
        out_shape=jax.ShapeDtypeStruct((block, block), jnp.float32),
        in_specs=[pl.BlockSpec(memory_space=pltpu.VMEM)] * 5,
        out_specs=pl.BlockSpec(memory_space=pltpu.VMEM),
        cost_estimate=pl.CostEstimate(
            flops=flops, transcendentals=0, bytes_accessed=4 * (block * block + block * depth) + 2 * (depth + width) * 256
        ),
    )(row_rev, col_pad, row_norm, col_norm, weights)


def shards(snapshots, offsets, window_len, cone_exp):
    block = snapshots.shape[0]
    lags = LAGS
    tail = snapshots[block - (lags - 1) :]
    history = shifted(tail, "col", 1)
    col_ext = jnp.concatenate([history, snapshots], axis=0)
    chosen = lax.dynamic_index_in_dim(offsets, lax.axis_index("row"), 0, keepdims=False)
    row_ext = broadcast_band(snapshots[block - lags :], snapshots, chosen)[1:]
    row_begin = chosen * block
    col_begin = lax.axis_index("col") * block
    extent = block + lags
    row_lengths = lax.dynamic_slice_in_dim(window_len, row_begin, block)
    row_exps = lax.dynamic_slice_in_dim(cone_exp, row_begin, block)
    row_weights = reversed_cone(row_lengths, row_exps, lags, extent)
    col_weights = cone_matrix(
        lax.dynamic_slice_in_dim(window_len, col_begin, block),
        lax.dynamic_slice_in_dim(cone_exp, col_begin, block),
        lags,
    )
    row_wide = row_ext.astype(jnp.float32)
    col_wide = col_ext.astype(jnp.float32)
    row_part = jnp.sum(row_wide * row_wide, axis=1)
    col_part = jnp.sum(col_wide * col_wide, axis=1)
    row_rev = jnp.pad(row_ext[::-1], ((extent - row_ext.shape[0], 0), (0, 0)))
    row_part_rev = jnp.pad(row_part[::-1], (extent - row_ext.shape[0], 0))
    width = 2 * block
    col_pad = jnp.pad(col_ext, ((0, width - col_ext.shape[0]), (0, 0)))
    col_part_pad = jnp.pad(col_part, (0, width - col_ext.shape[0]))
    total = lag_total(row_rev, col_pad, row_part_rev[:, None], col_part_pad[None, :], row_weights, block, lags)
    row_sum = jnp.dot(row_weights, row_part_rev, precision=lax.Precision.HIGHEST, preferred_element_type=jnp.float32)
    col_sum = jnp.dot(col_weights, col_part, precision=lax.Precision.HIGHEST, preferred_element_type=jnp.float32)
    n_chan = lax.axis_size("chan")
    share = block // n_chan
    tiles = total.reshape(n_chan, share, block)
    col_rows = jnp.broadcast_to(col_sum[None, None, :], (n_chan, 1, block))
    row_rows = jnp.pad(row_sum.reshape(n_chan, 1, share), ((0, 0), (0, 6), (0, block - share)))
    payload = jnp.concatenate([tiles, col_rows, row_rows], axis=1).reshape(n_chan * (share + 8), block)
    mine = lax.psum_scatter(payload, "chan", scatter_dimension=0, tiled=True)
    row_scale = jnp.sqrt(mine[share + 1, :share] / C + epsilon)
    col_scale = jnp.sqrt(mine[share] / C + epsilon)
    return jnp.exp(-mine[:share] / (2.0 * C * row_scale[:, None] * col_scale[None, :]))


def solution(mesh):
    in_specs = (P("col", "chan"), P(), P(), P())
    out_specs = P(("row", "chan"), "col")
    return jax.shard_map(shards, mesh=mesh, in_specs=in_specs, out_specs=out_specs, check_vma=False)
```

```python
import functools

import jax
import jax.numpy as jnp
from jax import lax
from jax.experimental import pallas as pl
from jax.experimental.pallas import tpu as pltpu
from jax.sharding import PartitionSpec as P

C = 2048
LAGS = 256


epsilon = 1e-05


def shifted(block, axis, distance):
    devices = range(lax.axis_size(axis))
    route = [((i - distance) % len(devices), i) for i in devices]
    return lax.ppermute(block, axis, route)


def spread(value, axis, source):
    kept = jnp.where(lax.axis_index(axis) == source, value, 0).astype(value.dtype)
    return lax.psum(kept, axis)


COL_PARTS = (2, 4, 2)


def col_route(step):
    outer, mid, inner = COL_PARTS
    route = []
    for c in range(outer * mid * inner):
        z, x, k = c // (mid * inner), (c // inner) % mid, c % inner
        z, x, k = step(z, x, k)
        route.append((c, (z % outer * mid + x % mid) * inner + k % inner))
    return route


def broadcast_band(tail, block, source):
    outer, mid, inner = COL_PARTS
    count = outer * mid * inner
    rows_total = tail.shape[0] + block.shape[0]
    if lax.axis_size("col") != count or mid != 4 or outer != 2 or inner != 2 or rows_total % 4 != 0:
        joined = jnp.concatenate([shifted(tail, "col", 1), block], axis=0)
        return spread(joined, "col", source)
    me = lax.axis_index("col")
    value = jnp.concatenate([tail, block], axis=0)
    split = tail.shape[0]
    half = rows_total // 2
    quarter = half // 2

    def deltas(origin):
        dz = (me // (mid * inner) - origin // (mid * inner)) % outer
        dx = ((me // inner) % mid - (origin // inner) % mid) % mid
        dk = (me % inner - origin % inner) % inner
        return dz, dx, dk

    tz, tx, tk = deltas((source + count - 1) % count)
    bz, bx, bk = deltas(source)
    core = me % inner
    start = core * half
    rows = start + lax.broadcasted_iota(jnp.int32, (half, 1), 0)

    def pick(tail_test, block_test):
        return jnp.where(rows < split, tail_test, block_test)

    flip = col_route(lambda z, x, k: (z, x, k + 1))
    wanted = lax.dynamic_slice_in_dim(value, (1 - core) * half, half)
    got = lax.ppermute(wanted, "col", flip)
    mine = jnp.where(pick(tk == 1, bk == 1), got, lax.dynamic_slice_in_dim(value, start, half))
    plus = col_route(lambda z, x, k: (z, x + 1, k))
    minus = col_route(lambda z, x, k: (z, x - 1, k))
    from_left = lax.ppermute(mine, "col", plus)
    from_right = lax.ppermute(mine, "col", minus)
    mine = jnp.where(pick(tx == 1, bx == 1), from_left, jnp.where(pick(tx == 3, bx == 3), from_right, mine))
    first = lax.ppermute(mine[:quarter], "col", plus)
    second = lax.ppermute(mine[quarter:], "col", minus)
    mine = jnp.where(pick(tx == 2, bx == 2), jnp.concatenate([first, second], axis=0), mine)
    got = lax.ppermute(mine, "col", col_route(lambda z, x, k: (z + 1, x, k)))
    mine = jnp.where(pick(tz == 1, bz == 1), got, mine)
    other = lax.ppermute(mine, "col", flip)
    return jnp.where(core == 0, jnp.concatenate([mine, other], axis=0), jnp.concatenate([other, mine], axis=0))


def broadcast_pieces(tail, block, source):
    count = lax.axis_size("col")
    value = jnp.concatenate([tail, block], axis=0)
    rows_total = value.shape[0]
    if rows_total % count != 0:
        joined = jnp.concatenate([shifted(tail, "col", 1), block], axis=0)
        return spread(joined, "col", source)
    piece = rows_total // count
    split = tail.shape[0]
    parts = value.reshape(count, piece, value.shape[1])
    got = lax.all_to_all(parts, "col", 0, 0, tiled=False)
    me = lax.axis_index("col")
    rows = me * piece + lax.broadcasted_iota(jnp.int32, (piece, 1), 0)
    early = lax.dynamic_index_in_dim(got, (source + count - 1) % count, 0, keepdims=False)
    late = lax.dynamic_index_in_dim(got, source, 0, keepdims=False)
    mine = jnp.where(rows < split, early, late)
    spread_out = jnp.broadcast_to(mine[None], (count, piece, value.shape[1]))
    full = lax.all_to_all(spread_out, "col", 0, 0, tiled=False)
    return full.reshape(rows_total, value.shape[1])


def power_int(frac, exps):
    square = frac * frac
    return jnp.where(
        exps == 0,
        jnp.ones_like(frac),
        jnp.where(exps == 1, frac, jnp.where(exps == 2, square, square * frac)),
    )


def cone_matrix(lengths, exps, lags):
    rows = lengths.shape[0]
    row_pos = lax.broadcasted_iota(jnp.int32, (rows, rows + lags - 1), 0)
    col_pos = lax.broadcasted_iota(jnp.int32, (rows, rows + lags - 1), 1)
    lag = row_pos + (lags - 1) - col_pos
    span = lengths[:, None]
    valid = (lag >= 0) & (lag < span)
    frac = (span.astype(jnp.float32) - lag.astype(jnp.float32)) / span.astype(jnp.float32)
    cone = jnp.where(valid, power_int(frac, exps[:, None]), jnp.zeros_like(frac))
    return cone / jnp.sum(cone, axis=1, keepdims=True)


def reversed_cone(lengths, exps, lags, depth):
    rows = lengths.shape[0]
    row_pos = lax.broadcasted_iota(jnp.int32, (rows, depth), 0)
    col_pos = lax.broadcasted_iota(jnp.int32, (rows, depth), 1)
    lag = row_pos + col_pos - (depth - lags)
    span = lengths[:, None]
    valid = (lag >= 0) & (lag < span)
    frac = (span.astype(jnp.float32) - lag.astype(jnp.float32)) / span.astype(jnp.float32)
    cone = jnp.where(valid, power_int(frac, exps[:, None]), jnp.zeros_like(frac))
    return cone / jnp.sum(cone, axis=1, keepdims=True)


def lag_kernel(lags, r_ref, q_ref, rp_ref, cp_ref, w_ref, o_ref):
    inner = lax.dot_general(
        r_ref[...], q_ref[...], (((1,), (1,)), ((), ())), preferred_element_type=jnp.float32
    )
    dist = rp_ref[...] + cp_ref[...] - 2.0 * inner
    width = dist.shape[1]
    depth = dist.shape[0]
    skew = pltpu.roll(dist, width - lags, 1, stride=1, stride_axis=0)
    block = o_ref.shape[1]
    chunk = 128
    band = chunk + lags
    span = block + chunk
    for m in range(o_ref.shape[0] // chunk):
        low = depth - band - chunk * m
        part = jnp.dot(
            w_ref[chunk * m : chunk * (m + 1), low : low + band],
            skew[low : low + band, low : low + span],
            precision=lax.Precision.HIGHEST,
            preferred_element_type=jnp.float32,
        )
        lined = pltpu.roll(part, span - (chunk - 1), 1, stride=1, stride_axis=0)
        o_ref[chunk * m : chunk * (m + 1), :] = lined[:, :block]


def lag_total(row_rev, col_pad, row_norm, col_norm, weights, block, lags):
    depth = row_rev.shape[0]
    width = col_pad.shape[0]
    flops = 2 * depth * width * row_rev.shape[1] + 6 * 2 * block * (128 + lags) * (block + 128)
    return pl.pallas_call(
        functools.partial(lag_kernel, lags),
        out_shape=jax.ShapeDtypeStruct((block, block), jnp.float32),
        in_specs=[pl.BlockSpec(memory_space=pltpu.VMEM)] * 5,
        out_specs=pl.BlockSpec(memory_space=pltpu.VMEM),
        cost_estimate=pl.CostEstimate(
            flops=flops, transcendentals=0, bytes_accessed=4 * (block * block + block * depth) + 2 * (depth + width) * 256
        ),
    )(row_rev, col_pad, row_norm, col_norm, weights)


def shards(snapshots, offsets, window_len, cone_exp):
    block = snapshots.shape[0]
    lags = LAGS
    tail = snapshots[block - (lags - 1) :]
    history = shifted(tail, "col", 1)
    col_ext = jnp.concatenate([history, snapshots], axis=0)
    chosen = lax.dynamic_index_in_dim(offsets, lax.axis_index("row"), 0, keepdims=False)
    row_ext = broadcast_pieces(snapshots[block - lags :], snapshots, chosen)[1:]
    row_begin = chosen * block
    col_begin = lax.axis_index("col") * block
    extent = block + lags
    row_lengths = lax.dynamic_slice_in_dim(window_len, row_begin, block)
    row_exps = lax.dynamic_slice_in_dim(cone_exp, row_begin, block)
    row_weights = reversed_cone(row_lengths, row_exps, lags, extent)
    col_weights = cone_matrix(
        lax.dynamic_slice_in_dim(window_len, col_begin, block),
        lax.dynamic_slice_in_dim(cone_exp, col_begin, block),
        lags,
    )
    row_wide = row_ext.astype(jnp.float32)
    col_wide = col_ext.astype(jnp.float32)
    row_part = jnp.sum(row_wide * row_wide, axis=1)
    col_part = jnp.sum(col_wide * col_wide, axis=1)
    row_rev = jnp.pad(row_ext[::-1], ((extent - row_ext.shape[0], 0), (0, 0)))
    row_part_rev = jnp.pad(row_part[::-1], (extent - row_ext.shape[0], 0))
    width = 2 * block
    col_pad = jnp.pad(col_ext, ((0, width - col_ext.shape[0]), (0, 0)))
    col_part_pad = jnp.pad(col_part, (0, width - col_ext.shape[0]))
    total = lag_total(row_rev, col_pad, row_part_rev[:, None], col_part_pad[None, :], row_weights, block, lags)
    row_sum = jnp.dot(row_weights, row_part_rev, precision=lax.Precision.HIGHEST, preferred_element_type=jnp.float32)
    col_sum = jnp.dot(col_weights, col_part, precision=lax.Precision.HIGHEST, preferred_element_type=jnp.float32)
    n_chan = lax.axis_size("chan")
    share = block // n_chan
    tiles = total.reshape(n_chan, share, block)
    col_rows = jnp.broadcast_to(col_sum[None, None, :], (n_chan, 1, block))
    row_rows = jnp.pad(row_sum.reshape(n_chan, 1, share), ((0, 0), (0, 6), (0, block - share)))
    payload = jnp.concatenate([tiles, col_rows, row_rows], axis=1).reshape(n_chan * (share + 8), block)
    mine = lax.psum_scatter(payload, "chan", scatter_dimension=0, tiled=True)
    row_scale = jnp.sqrt(mine[share + 1, :share] / C + epsilon)
    col_scale = jnp.sqrt(mine[share] / C + epsilon)
    return jnp.exp(-mine[:share] / (2.0 * C * row_scale[:, None] * col_scale[None, :]))


def solution(mesh):
    in_specs = (P("col", "chan"), P(), P(), P())
    out_specs = P(("row", "chan"), "col")
    return jax.shard_map(shards, mesh=mesh, in_specs=in_specs, out_specs=out_specs, check_vma=False)
```

```python
import functools

import jax
import jax.numpy as jnp
from jax import lax
from jax.experimental import pallas as pl
from jax.experimental.pallas import tpu as pltpu
from jax.sharding import PartitionSpec as P

C = 2048
LAGS = 256


epsilon = 1e-05


def shifted(block, axis, distance):
    devices = range(lax.axis_size(axis))
    route = [((i - distance) % len(devices), i) for i in devices]
    return lax.ppermute(block, axis, route)


def spread(value, axis, source):
    kept = jnp.where(lax.axis_index(axis) == source, value, 0).astype(value.dtype)
    return lax.psum(kept, axis)


COL_PARTS = (2, 4, 2)


def col_route(step):
    outer, mid, inner = COL_PARTS
    route = []
    for c in range(outer * mid * inner):
        z, x, k = c // (mid * inner), (c // inner) % mid, c % inner
        z, x, k = step(z, x, k)
        route.append((c, (z % outer * mid + x % mid) * inner + k % inner))
    return route


def broadcast_band(tail, block, source):
    outer, mid, inner = COL_PARTS
    count = outer * mid * inner
    rows_total = tail.shape[0] + block.shape[0]
    if lax.axis_size("col") != count or mid != 4 or outer != 2 or inner != 2 or rows_total % 4 != 0:
        joined = jnp.concatenate([shifted(tail, "col", 1), block], axis=0)
        return spread(joined, "col", source)
    me = lax.axis_index("col")
    value = jnp.concatenate([tail, block], axis=0)
    split = tail.shape[0]
    half = rows_total // 2
    quarter = half // 2

    def deltas(origin):
        dz = (me // (mid * inner) - origin // (mid * inner)) % outer
        dx = ((me // inner) % mid - (origin // inner) % mid) % mid
        dk = (me % inner - origin % inner) % inner
        return dz, dx, dk

    tz, tx, tk = deltas((source + count - 1) % count)
    bz, bx, bk = deltas(source)
    core = me % inner
    start = core * half
    rows = start + lax.broadcasted_iota(jnp.int32, (half, 1), 0)

    def pick(tail_test, block_test):
        return jnp.where(rows < split, tail_test, block_test)

    flip = col_route(lambda z, x, k: (z, x, k + 1))
    wanted = lax.dynamic_slice_in_dim(value, (1 - core) * half, half)
    got = lax.ppermute(wanted, "col", flip)
    mine = jnp.where(pick(tk == 1, bk == 1), got, lax.dynamic_slice_in_dim(value, start, half))
    plus = col_route(lambda z, x, k: (z, x + 1, k))
    minus = col_route(lambda z, x, k: (z, x - 1, k))
    from_left = lax.ppermute(mine, "col", plus)
    from_right = lax.ppermute(mine, "col", minus)
    mine = jnp.where(pick(tx == 1, bx == 1), from_left, jnp.where(pick(tx == 3, bx == 3), from_right, mine))
    first = lax.ppermute(mine[:quarter], "col", plus)
    second = lax.ppermute(mine[quarter:], "col", minus)
    mine = jnp.where(pick(tx == 2, bx == 2), jnp.concatenate([first, second], axis=0), mine)
    got = lax.ppermute(mine, "col", col_route(lambda z, x, k: (z + 1, x, k)))
    mine = jnp.where(pick(tz == 1, bz == 1), got, mine)
    other = lax.ppermute(mine, "col", flip)
    return jnp.where(core == 0, jnp.concatenate([mine, other], axis=0), jnp.concatenate([other, mine], axis=0))


def broadcast_pieces(tail, block, source):
    count = lax.axis_size("col")
    value = jnp.concatenate([tail, block], axis=0)
    rows_total = value.shape[0]
    if rows_total % count != 0:
        joined = jnp.concatenate([shifted(tail, "col", 1), block], axis=0)
        return spread(joined, "col", source)
    piece = rows_total // count
    split = tail.shape[0]
    parts = value.reshape(count, piece, value.shape[1])
    got = lax.all_to_all(parts, "col", 0, 0, tiled=False)
    me = lax.axis_index("col")
    rows = me * piece + lax.broadcasted_iota(jnp.int32, (piece, 1), 0)
    early = lax.dynamic_index_in_dim(got, (source + count - 1) % count, 0, keepdims=False)
    late = lax.dynamic_index_in_dim(got, source, 0, keepdims=False)
    mine = jnp.where(rows < split, early, late)
    spread_out = jnp.broadcast_to(mine[None], (count, piece, value.shape[1]))
    full = lax.all_to_all(spread_out, "col", 0, 0, tiled=False)
    return full.reshape(rows_total, value.shape[1])


def power_int(frac, exps):
    square = frac * frac
    return jnp.where(
        exps == 0,
        jnp.ones_like(frac),
        jnp.where(exps == 1, frac, jnp.where(exps == 2, square, square * frac)),
    )


def cone_matrix(lengths, exps, lags):
    rows = lengths.shape[0]
    row_pos = lax.broadcasted_iota(jnp.int32, (rows, rows + lags - 1), 0)
    col_pos = lax.broadcasted_iota(jnp.int32, (rows, rows + lags - 1), 1)
    lag = row_pos + (lags - 1) - col_pos
    span = lengths[:, None]
    valid = (lag >= 0) & (lag < span)
    frac = (span.astype(jnp.float32) - lag.astype(jnp.float32)) / span.astype(jnp.float32)
    cone = jnp.where(valid, power_int(frac, exps[:, None]), jnp.zeros_like(frac))
    return cone / jnp.sum(cone, axis=1, keepdims=True)


def reversed_cone(lengths, exps, lags, depth):
    rows = lengths.shape[0]
    row_pos = lax.broadcasted_iota(jnp.int32, (rows, depth), 0)
    col_pos = lax.broadcasted_iota(jnp.int32, (rows, depth), 1)
    lag = row_pos + col_pos - (depth - lags)
    span = lengths[:, None]
    valid = (lag >= 0) & (lag < span)
    frac = (span.astype(jnp.float32) - lag.astype(jnp.float32)) / span.astype(jnp.float32)
    cone = jnp.where(valid, power_int(frac, exps[:, None]), jnp.zeros_like(frac))
    return cone / jnp.sum(cone, axis=1, keepdims=True)


def lag_kernel(lags, r_ref, q_ref, rp_ref, cp_ref, w_ref, o_ref):
    inner = lax.dot_general(
        r_ref[...], q_ref[...], (((1,), (1,)), ((), ())), preferred_element_type=jnp.float32
    )
    dist = rp_ref[...] + cp_ref[...] - 2.0 * inner
    width = dist.shape[1]
    depth = dist.shape[0]
    skew = pltpu.roll(dist, width - lags, 1, stride=1, stride_axis=0)
    block = o_ref.shape[1]
    chunk = 128
    band = chunk + lags
    span = block + chunk
    for m in range(o_ref.shape[0] // chunk):
        low = depth - band - chunk * m
        part = jnp.dot(
            w_ref[chunk * m : chunk * (m + 1), low : low + band],
            skew[low : low + band, low : low + span],
            precision=lax.Precision.HIGHEST,
            preferred_element_type=jnp.float32,
        )
        lined = pltpu.roll(part, span - (chunk - 1), 1, stride=1, stride_axis=0)
        o_ref[chunk * m : chunk * (m + 1), :] = lined[:, :block]


def lag_total(row_rev, col_pad, row_norm, col_norm, weights, block, lags):
    depth = row_rev.shape[0]
    width = col_pad.shape[0]
    flops = 2 * depth * width * row_rev.shape[1] + 6 * 2 * block * (128 + lags) * (block + 128)
    return pl.pallas_call(
        functools.partial(lag_kernel, lags),
        out_shape=jax.ShapeDtypeStruct((block, block), jnp.float32),
        in_specs=[pl.BlockSpec(memory_space=pltpu.VMEM)] * 5,
        out_specs=pl.BlockSpec(memory_space=pltpu.VMEM),
        cost_estimate=pl.CostEstimate(
            flops=flops, transcendentals=0, bytes_accessed=4 * (block * block + block * depth) + 2 * (depth + width) * 256
        ),
    )(row_rev, col_pad, row_norm, col_norm, weights)


def shards(snapshots, offsets, window_len, cone_exp):
    block = snapshots.shape[0]
    lags = LAGS
    tail = snapshots[block - (lags - 1) :]
    history = shifted(tail, "col", 1)
    col_ext = jnp.concatenate([history, snapshots], axis=0)
    chosen = lax.dynamic_index_in_dim(offsets, lax.axis_index("row"), 0, keepdims=False)
    row_ext = broadcast_pieces(snapshots[block - lags :], snapshots, chosen)[1:]
    row_begin = chosen * block
    col_begin = lax.axis_index("col") * block
    extent = block + lags
    row_lengths = lax.dynamic_slice_in_dim(window_len, row_begin, block)
    row_exps = lax.dynamic_slice_in_dim(cone_exp, row_begin, block)
    row_weights = reversed_cone(row_lengths, row_exps, lags, extent)
    col_weights = cone_matrix(
        lax.dynamic_slice_in_dim(window_len, col_begin, block),
        lax.dynamic_slice_in_dim(cone_exp, col_begin, block),
        lags,
    )
    row_wide = row_ext.astype(jnp.float32)
    col_wide = col_ext.astype(jnp.float32)
    row_part = jnp.sum(row_wide * row_wide, axis=1)
    col_part = jnp.sum(col_wide * col_wide, axis=1)
    row_rev = jnp.pad(row_ext[::-1], ((extent - row_ext.shape[0], 0), (0, 0)))
    row_part_rev = jnp.pad(row_part[::-1], (extent - row_ext.shape[0], 0))
    width = 2 * block
    col_pad = jnp.pad(col_ext, ((0, width - col_ext.shape[0]), (0, 0)))
    col_part_pad = jnp.pad(col_part, (0, width - col_ext.shape[0]))
    total = lag_total(row_rev, col_pad, row_part_rev[:, None], col_part_pad[None, :], row_weights, block, lags)
    row_sum = jnp.dot(row_weights, row_part_rev, precision=lax.Precision.HIGHEST, preferred_element_type=jnp.float32)
    col_sum = jnp.dot(col_weights, col_part, precision=lax.Precision.HIGHEST, preferred_element_type=jnp.float32)
    n_chan = lax.axis_size("chan")
    share = block // n_chan
    tiles = total.reshape(n_chan, share, block)
    col_rows = jnp.broadcast_to(col_sum[None, None, :], (n_chan, 1, block))
    row_rows = jnp.pad(row_sum.reshape(n_chan, 1, share), ((0, 0), (0, 6), (0, block - share)))
    payload = jnp.concatenate([tiles, col_rows, row_rows], axis=1)
    mine = jnp.sum(lax.all_to_all(payload, "chan", 0, 0, tiled=False), axis=0)
    row_scale = jnp.sqrt(mine[share + 1, :share] / C + epsilon)
    col_scale = jnp.sqrt(mine[share] / C + epsilon)
    return jnp.exp(-mine[:share] / (2.0 * C * row_scale[:, None] * col_scale[None, :]))


def solution(mesh):
    in_specs = (P("col", "chan"), P(), P(), P())
    out_specs = P(("row", "chan"), "col")
    return jax.shard_map(shards, mesh=mesh, in_specs=in_specs, out_specs=out_specs, check_vma=False)
```

```python
import functools

import jax
import jax.numpy as jnp
from jax import lax
from jax.experimental import pallas as pl
from jax.experimental.pallas import tpu as pltpu
from jax.sharding import PartitionSpec as P

C = 2048
LAGS = 256


epsilon = 1e-05


def shifted(block, axis, distance):
    devices = range(lax.axis_size(axis))
    route = [((i - distance) % len(devices), i) for i in devices]
    return lax.ppermute(block, axis, route)


def spread(value, axis, source):
    kept = jnp.where(lax.axis_index(axis) == source, value, 0).astype(value.dtype)
    return lax.psum(kept, axis)


COL_PARTS = (2, 4, 2)


def col_route(step):
    outer, mid, inner = COL_PARTS
    route = []
    for c in range(outer * mid * inner):
        z, x, k = c // (mid * inner), (c // inner) % mid, c % inner
        z, x, k = step(z, x, k)
        route.append((c, (z % outer * mid + x % mid) * inner + k % inner))
    return route


def broadcast_band(tail, block, source):
    outer, mid, inner = COL_PARTS
    count = outer * mid * inner
    rows_total = tail.shape[0] + block.shape[0]
    if lax.axis_size("col") != count or mid != 4 or outer != 2 or inner != 2 or rows_total % 4 != 0:
        joined = jnp.concatenate([shifted(tail, "col", 1), block], axis=0)
        return spread(joined, "col", source)
    me = lax.axis_index("col")
    value = jnp.concatenate([tail, block], axis=0)
    split = tail.shape[0]
    half = rows_total // 2
    quarter = half // 2

    def deltas(origin):
        dz = (me // (mid * inner) - origin // (mid * inner)) % outer
        dx = ((me // inner) % mid - (origin // inner) % mid) % mid
        dk = (me % inner - origin % inner) % inner
        return dz, dx, dk

    tz, tx, tk = deltas((source + count - 1) % count)
    bz, bx, bk = deltas(source)
    core = me % inner
    start = core * half
    rows = start + lax.broadcasted_iota(jnp.int32, (half, 1), 0)

    def pick(tail_test, block_test):
        return jnp.where(rows < split, tail_test, block_test)

    flip = col_route(lambda z, x, k: (z, x, k + 1))
    wanted = lax.dynamic_slice_in_dim(value, (1 - core) * half, half)
    got = lax.ppermute(wanted, "col", flip)
    mine = jnp.where(pick(tk == 1, bk == 1), got, lax.dynamic_slice_in_dim(value, start, half))
    plus = col_route(lambda z, x, k: (z, x + 1, k))
    minus = col_route(lambda z, x, k: (z, x - 1, k))
    from_left = lax.ppermute(mine, "col", plus)
    from_right = lax.ppermute(mine, "col", minus)
    mine = jnp.where(pick(tx == 1, bx == 1), from_left, jnp.where(pick(tx == 3, bx == 3), from_right, mine))
    first = lax.ppermute(mine[:quarter], "col", plus)
    second = lax.ppermute(mine[quarter:], "col", minus)
    mine = jnp.where(pick(tx == 2, bx == 2), jnp.concatenate([first, second], axis=0), mine)
    got = lax.ppermute(mine, "col", col_route(lambda z, x, k: (z + 1, x, k)))
    mine = jnp.where(pick(tz == 1, bz == 1), got, mine)
    other = lax.ppermute(mine, "col", flip)
    return jnp.where(core == 0, jnp.concatenate([mine, other], axis=0), jnp.concatenate([other, mine], axis=0))


def broadcast_block(block, source):
    count = lax.axis_size("col")
    piece = block.shape[0] // count
    parts = block.reshape(count, piece, block.shape[1])
    got = lax.all_to_all(parts, "col", 0, 0, tiled=False)
    early = lax.dynamic_index_in_dim(got, (source + count - 1) % count, 0, keepdims=False)
    late = lax.dynamic_index_in_dim(got, source, 0, keepdims=False)
    pair = jnp.stack([early, late])
    spread_out = jnp.broadcast_to(pair[None], (count,) + pair.shape)
    return lax.all_to_all(spread_out, "col", 0, 0, tiled=False)


def power_int(frac, exps):
    square = frac * frac
    return jnp.where(
        exps == 0,
        jnp.ones_like(frac),
        jnp.where(exps == 1, frac, jnp.where(exps == 2, square, square * frac)),
    )


def cone_matrix(lengths, exps, lags):
    rows = lengths.shape[0]
    row_pos = lax.broadcasted_iota(jnp.int32, (rows, rows + lags - 1), 0)
    col_pos = lax.broadcasted_iota(jnp.int32, (rows, rows + lags - 1), 1)
    lag = row_pos + (lags - 1) - col_pos
    span = lengths[:, None]
    valid = (lag >= 0) & (lag < span)
    frac = (span.astype(jnp.float32) - lag.astype(jnp.float32)) / span.astype(jnp.float32)
    cone = jnp.where(valid, power_int(frac, exps[:, None]), jnp.zeros_like(frac))
    return cone / jnp.sum(cone, axis=1, keepdims=True)


def reversed_cone(lengths, exps, lags, depth):
    rows = lengths.shape[0]
    row_pos = lax.broadcasted_iota(jnp.int32, (rows, depth), 0)
    col_pos = lax.broadcasted_iota(jnp.int32, (rows, depth), 1)
    lag = row_pos + col_pos - (depth - lags) + 1
    span = lengths[:, None]
    valid = (lag >= 0) & (lag < span)
    frac = (span.astype(jnp.float32) - lag.astype(jnp.float32)) / span.astype(jnp.float32)
    cone = jnp.where(valid, power_int(frac, exps[:, None]), jnp.zeros_like(frac))
    return cone / jnp.sum(cone, axis=1, keepdims=True)


def lag_kernel(lags, r_ref, q_ref, cp_ref, csum_ref, w_ref, o_ref):
    rows = r_ref[...]
    wide = rows.astype(jnp.float32)
    square = wide * wide
    row_norm = jnp.sum(square, axis=1, keepdims=True)
    inner = lax.dot_general(
        rows, q_ref[...], (((1,), (1,)), ((), ())), preferred_element_type=jnp.float32
    )
    dist = row_norm + cp_ref[...] - 2.0 * inner
    width = dist.shape[1]
    depth = dist.shape[0]
    skew = pltpu.roll(dist, width - lags + 1, 1, stride=1, stride_axis=0)
    ones = jnp.ones((8, square.shape[1]), jnp.float32)
    norm_rows = lax.dot_general(
        ones, square, (((1,), (1,)), ((), ())), precision=lax.Precision.HIGHEST,
        preferred_element_type=jnp.float32,
    )
    row_sum = lax.dot_general(
        norm_rows, w_ref[...], (((1,), (1,)), ((), ())), precision=lax.Precision.HIGHEST,
        preferred_element_type=jnp.float32,
    )
    count, share, block = o_ref.shape[0], 64, o_ref.shape[2]
    share = block // count
    chunk = 128
    band = chunk + lags
    span = block + chunk
    for m in range(block // chunk):
        low = depth - band - chunk * m
        part = jnp.dot(
            w_ref[chunk * m : chunk * (m + 1), low : low + band],
            skew[low : low + band, low : low + span],
            precision=lax.Precision.HIGHEST,
            preferred_element_type=jnp.float32,
        )
        lined = pltpu.roll(part, span - (chunk - 1), 1, stride=1, stride_axis=0)
        for h in range(chunk // share):
            o_ref[(chunk * m) // share + h, 0:share, :] = lined[share * h : share * (h + 1), :block]
    extra = o_ref.shape[1] - share
    tail_rows = jnp.concatenate(
        [csum_ref[...], row_sum[0:1, :], jnp.zeros((extra - 2, block), jnp.float32)], axis=0
    )
    for k in range(count):
        o_ref[k, share:, :] = tail_rows


def lag_total(row_rev, col_pad, col_norm, col_sum, weights, count, lags):
    depth = row_rev.shape[0]
    width = col_pad.shape[0]
    block = weights.shape[0]
    share = block // count
    flops = 2 * depth * width * row_rev.shape[1] + 6 * 2 * block * (128 + lags) * (block + 128)
    return pl.pallas_call(
        functools.partial(lag_kernel, lags),
        out_shape=jax.ShapeDtypeStruct((count, share + 8, block), jnp.float32),
        in_specs=[pl.BlockSpec(memory_space=pltpu.VMEM)] * 5,
        out_specs=pl.BlockSpec(memory_space=pltpu.VMEM),
        cost_estimate=pl.CostEstimate(
            flops=flops, transcendentals=0, bytes_accessed=4 * (block * block + block * depth) + 2 * (depth + width) * 256
        ),
    )(row_rev, col_pad, col_norm, col_sum, weights)


def shards(snapshots, offsets, window_len, cone_exp):
    block = snapshots.shape[0]
    lags = LAGS
    count = lax.axis_size("col")
    tail = snapshots[block - (lags - 1) :]
    history = shifted(tail, "col", 1)
    col_ext = jnp.concatenate([history, snapshots], axis=0)
    chosen = lax.dynamic_index_in_dim(offsets, lax.axis_index("row"), 0, keepdims=False)
    pieces = broadcast_block(snapshots, chosen)
    piece = block // count
    band_rows = pieces[:, 1].reshape(block, snapshots.shape[1])
    tail_rows = pieces[count - lags // piece :, 0].reshape(lags, snapshots.shape[1])
    row_rev = jnp.concatenate([tail_rows, band_rows], axis=0)[::-1]
    row_begin = chosen * block
    col_begin = lax.axis_index("col") * block
    extent = block + lags
    row_lengths = lax.dynamic_slice_in_dim(window_len, row_begin, block)
    row_exps = lax.dynamic_slice_in_dim(cone_exp, row_begin, block)
    row_weights = reversed_cone(row_lengths, row_exps, lags, extent)
    col_weights = cone_matrix(
        lax.dynamic_slice_in_dim(window_len, col_begin, block),
        lax.dynamic_slice_in_dim(cone_exp, col_begin, block),
        lags,
    )
    col_wide = col_ext.astype(jnp.float32)
    col_part = jnp.sum(col_wide * col_wide, axis=1)
    width = 2 * block
    col_pad = jnp.pad(col_ext, ((0, width - col_ext.shape[0]), (0, 0)))
    col_part_pad = jnp.pad(col_part, (0, width - col_ext.shape[0]))
    col_sum = jnp.dot(col_weights, col_part, precision=lax.Precision.HIGHEST, preferred_element_type=jnp.float32)
    n_chan = lax.axis_size("chan")
    share = block // n_chan
    payload = lag_total(row_rev, col_pad, col_part_pad[None, :], col_sum[None, :], row_weights, n_chan, lags)
    mine = jnp.sum(lax.all_to_all(payload, "chan", 0, 0, tiled=False), axis=0)
    row_sum = lax.dynamic_slice_in_dim(mine[share + 1], lax.axis_index("chan") * share, share)
    row_scale = jnp.sqrt(row_sum / C + epsilon)
    col_scale = jnp.sqrt(mine[share] / C + epsilon)
    return jnp.exp(-mine[:share] / (2.0 * C * row_scale[:, None] * col_scale[None, :]))


def solution(mesh):
    in_specs = (P("col", "chan"), P(), P(), P())
    out_specs = P(("row", "chan"), "col")
    return jax.shard_map(shards, mesh=mesh, in_specs=in_specs, out_specs=out_specs, check_vma=False)
```

```python
import functools

import jax
import jax.numpy as jnp
from jax import lax
from jax.experimental import pallas as pl
from jax.experimental.pallas import tpu as pltpu
from jax.sharding import PartitionSpec as P

C = 2048
LAGS = 256


epsilon = 1e-05


def shifted(block, axis, distance):
    devices = range(lax.axis_size(axis))
    route = [((i - distance) % len(devices), i) for i in devices]
    return lax.ppermute(block, axis, route)


def spread(value, axis, source):
    kept = jnp.where(lax.axis_index(axis) == source, value, 0).astype(value.dtype)
    return lax.psum(kept, axis)


COL_PARTS = (2, 4, 2)


def col_route(step):
    outer, mid, inner = COL_PARTS
    route = []
    for c in range(outer * mid * inner):
        z, x, k = c // (mid * inner), (c // inner) % mid, c % inner
        z, x, k = step(z, x, k)
        route.append((c, (z % outer * mid + x % mid) * inner + k % inner))
    return route


def broadcast_band(tail, block, source):
    outer, mid, inner = COL_PARTS
    count = outer * mid * inner
    rows_total = tail.shape[0] + block.shape[0]
    if lax.axis_size("col") != count or mid != 4 or outer != 2 or inner != 2 or rows_total % 4 != 0:
        joined = jnp.concatenate([shifted(tail, "col", 1), block], axis=0)
        return spread(joined, "col", source)
    me = lax.axis_index("col")
    value = jnp.concatenate([tail, block], axis=0)
    split = tail.shape[0]
    half = rows_total // 2
    quarter = half // 2

    def deltas(origin):
        dz = (me // (mid * inner) - origin // (mid * inner)) % outer
        dx = ((me // inner) % mid - (origin // inner) % mid) % mid
        dk = (me % inner - origin % inner) % inner
        return dz, dx, dk

    tz, tx, tk = deltas((source + count - 1) % count)
    bz, bx, bk = deltas(source)
    core = me % inner
    start = core * half
    rows = start + lax.broadcasted_iota(jnp.int32, (half, 1), 0)

    def pick(tail_test, block_test):
        return jnp.where(rows < split, tail_test, block_test)

    flip = col_route(lambda z, x, k: (z, x, k + 1))
    wanted = lax.dynamic_slice_in_dim(value, (1 - core) * half, half)
    got = lax.ppermute(wanted, "col", flip)
    mine = jnp.where(pick(tk == 1, bk == 1), got, lax.dynamic_slice_in_dim(value, start, half))
    plus = col_route(lambda z, x, k: (z, x + 1, k))
    minus = col_route(lambda z, x, k: (z, x - 1, k))
    from_left = lax.ppermute(mine, "col", plus)
    from_right = lax.ppermute(mine, "col", minus)
    mine = jnp.where(pick(tx == 1, bx == 1), from_left, jnp.where(pick(tx == 3, bx == 3), from_right, mine))
    first = lax.ppermute(mine[:quarter], "col", plus)
    second = lax.ppermute(mine[quarter:], "col", minus)
    mine = jnp.where(pick(tx == 2, bx == 2), jnp.concatenate([first, second], axis=0), mine)
    got = lax.ppermute(mine, "col", col_route(lambda z, x, k: (z + 1, x, k)))
    mine = jnp.where(pick(tz == 1, bz == 1), got, mine)
    other = lax.ppermute(mine, "col", flip)
    return jnp.where(core == 0, jnp.concatenate([mine, other], axis=0), jnp.concatenate([other, mine], axis=0))


def broadcast_block(block, source):
    count = lax.axis_size("col")
    piece = block.shape[0] // count
    parts = block.reshape(count, piece, block.shape[1])
    got = lax.all_to_all(parts, "col", 0, 0, tiled=False)
    early = lax.dynamic_index_in_dim(got, (source + count - 1) % count, 0, keepdims=False)
    late = lax.dynamic_index_in_dim(got, source, 0, keepdims=False)
    pair = jnp.stack([early, late])[:, ::-1]
    spread_out = jnp.broadcast_to(pair[None], (count,) + pair.shape)
    return lax.all_to_all(spread_out, "col", 0, 0, tiled=False)


def power_int(frac, exps):
    square = frac * frac
    return jnp.where(
        exps == 0,
        jnp.ones_like(frac),
        jnp.where(exps == 1, frac, jnp.where(exps == 2, square, square * frac)),
    )


def cone_matrix(lengths, exps, lags):
    rows = lengths.shape[0]
    row_pos = lax.broadcasted_iota(jnp.int32, (rows, rows + lags - 1), 0)
    col_pos = lax.broadcasted_iota(jnp.int32, (rows, rows + lags - 1), 1)
    lag = row_pos + (lags - 1) - col_pos
    span = lengths[:, None]
    valid = (lag >= 0) & (lag < span)
    frac = (span.astype(jnp.float32) - lag.astype(jnp.float32)) / span.astype(jnp.float32)
    cone = jnp.where(valid, power_int(frac, exps[:, None]), jnp.zeros_like(frac))
    return cone / jnp.sum(cone, axis=1, keepdims=True)


def reversed_cone(lengths, exps, lags, depth):
    rows = lengths.shape[0]
    row_pos = lax.broadcasted_iota(jnp.int32, (rows, depth), 0)
    col_pos = lax.broadcasted_iota(jnp.int32, (rows, depth), 1)
    lag = row_pos + col_pos - (depth - lags) + 1
    span = lengths[:, None]
    valid = (lag >= 0) & (lag < span)
    frac = (span.astype(jnp.float32) - lag.astype(jnp.float32)) / span.astype(jnp.float32)
    cone = jnp.where(valid, power_int(frac, exps[:, None]), jnp.zeros_like(frac))
    return cone / jnp.sum(cone, axis=1, keepdims=True)


def lag_kernel(lags, r_ref, q_ref, cp_ref, csum_ref, w_ref, o_ref):
    count = r_ref.shape[0]
    tail_count = lags // r_ref.shape[2]
    rows = jnp.concatenate(
        [r_ref[count - 1 - s, 1] for s in range(count)] + [r_ref[count - 1 - s, 0] for s in range(tail_count)],
        axis=0,
    )
    wide = rows.astype(jnp.float32)
    square = wide * wide
    row_norm = jnp.sum(square, axis=1, keepdims=True)
    inner = lax.dot_general(
        rows, q_ref[...], (((1,), (1,)), ((), ())), preferred_element_type=jnp.float32
    )
    dist = row_norm + cp_ref[...] - 2.0 * inner
    width = dist.shape[1]
    depth = dist.shape[0]
    skew = pltpu.roll(dist, width - lags + 1, 1, stride=1, stride_axis=0)
    ones = jnp.ones((8, square.shape[1]), jnp.float32)
    norm_rows = lax.dot_general(
        ones, square, (((1,), (1,)), ((), ())), precision=lax.Precision.HIGHEST,
        preferred_element_type=jnp.float32,
    )
    row_sum = lax.dot_general(
        norm_rows, w_ref[...], (((1,), (1,)), ((), ())), precision=lax.Precision.HIGHEST,
        preferred_element_type=jnp.float32,
    )
    count, share, block = o_ref.shape[0], 64, o_ref.shape[2]
    share = block // count
    chunk = 128
    band = chunk + lags
    span = block + chunk
    for m in range(block // chunk):
        low = depth - band - chunk * m
        part = jnp.dot(
            w_ref[chunk * m : chunk * (m + 1), low : low + band],
            skew[low : low + band, low : low + span],
            precision=lax.Precision.HIGHEST,
            preferred_element_type=jnp.float32,
        )
        lined = pltpu.roll(part, span - (chunk - 1), 1, stride=1, stride_axis=0)
        for h in range(chunk // share):
            o_ref[(chunk * m) // share + h, 0:share, :] = lined[share * h : share * (h + 1), :block]
    extra = o_ref.shape[1] - share
    tail_rows = jnp.concatenate(
        [csum_ref[...], row_sum[0:1, :], jnp.zeros((extra - 2, block), jnp.float32)], axis=0
    )
    for k in range(count):
        o_ref[k, share:, :] = tail_rows


def lag_total(row_rev, col_pad, col_norm, col_sum, weights, count, lags):
    depth = weights.shape[1]
    width = col_pad.shape[0]
    block = weights.shape[0]
    share = block // count
    flops = 2 * depth * width * col_pad.shape[1] + 6 * 2 * block * (128 + lags) * (block + 128)
    return pl.pallas_call(
        functools.partial(lag_kernel, lags),
        out_shape=jax.ShapeDtypeStruct((count, share + 8, block), jnp.float32),
        in_specs=[pl.BlockSpec(memory_space=pltpu.VMEM)] * 5,
        out_specs=pl.BlockSpec(memory_space=pltpu.VMEM),
        cost_estimate=pl.CostEstimate(
            flops=flops, transcendentals=0, bytes_accessed=4 * (block * block + block * depth) + 2 * (depth + width) * 256
        ),
    )(row_rev, col_pad, col_norm, col_sum, weights)


def shards(snapshots, offsets, window_len, cone_exp):
    block = snapshots.shape[0]
    lags = LAGS
    count = lax.axis_size("col")
    tail = snapshots[block - (lags - 1) :]
    history = shifted(tail, "col", 1)
    col_ext = jnp.concatenate([history, snapshots], axis=0)
    chosen = lax.dynamic_index_in_dim(offsets, lax.axis_index("row"), 0, keepdims=False)
    pieces = broadcast_block(snapshots, chosen)
    row_begin = chosen * block
    col_begin = lax.axis_index("col") * block
    extent = block + lags
    row_lengths = lax.dynamic_slice_in_dim(window_len, row_begin, block)
    row_exps = lax.dynamic_slice_in_dim(cone_exp, row_begin, block)
    row_weights = reversed_cone(row_lengths, row_exps, lags, extent)
    col_weights = cone_matrix(
        lax.dynamic_slice_in_dim(window_len, col_begin, block),
        lax.dynamic_slice_in_dim(cone_exp, col_begin, block),
        lags,
    )
    col_wide = col_ext.astype(jnp.float32)
    col_part = jnp.sum(col_wide * col_wide, axis=1)
    width = 2 * block
    col_pad = jnp.pad(col_ext, ((0, width - col_ext.shape[0]), (0, 0)))
    col_part_pad = jnp.pad(col_part, (0, width - col_ext.shape[0]))
    col_sum = jnp.dot(col_weights, col_part, precision=lax.Precision.HIGHEST, preferred_element_type=jnp.float32)
    n_chan = lax.axis_size("chan")
    share = block // n_chan
    payload = lag_total(pieces, col_pad, col_part_pad[None, :], col_sum[None, :], row_weights, n_chan, lags)
    mine = jnp.sum(lax.all_to_all(payload, "chan", 0, 0, tiled=False), axis=0)
    row_sum = lax.dynamic_slice_in_dim(mine[share + 1], lax.axis_index("chan") * share, share)
    row_scale = jnp.sqrt(row_sum / C + epsilon)
    col_scale = jnp.sqrt(mine[share] / C + epsilon)
    return jnp.exp(-mine[:share] / (2.0 * C * row_scale[:, None] * col_scale[None, :]))


def solution(mesh):
    in_specs = (P("col", "chan"), P(), P(), P())
    out_specs = P(("row", "chan"), "col")
    return jax.shard_map(shards, mesh=mesh, in_specs=in_specs, out_specs=out_specs, check_vma=False)
```

```python
import functools

import jax
import jax.numpy as jnp
from jax import lax
from jax.experimental import pallas as pl
from jax.experimental.pallas import tpu as pltpu
from jax.sharding import PartitionSpec as P

C = 2048
LAGS = 256


epsilon = 1e-05


def shifted(block, axis, distance):
    devices = range(lax.axis_size(axis))
    route = [((i - distance) % len(devices), i) for i in devices]
    return lax.ppermute(block, axis, route)


def spread(value, axis, source):
    kept = jnp.where(lax.axis_index(axis) == source, value, 0).astype(value.dtype)
    return lax.psum(kept, axis)


COL_PARTS = (2, 4, 2)


def col_route(step):
    outer, mid, inner = COL_PARTS
    route = []
    for c in range(outer * mid * inner):
        z, x, k = c // (mid * inner), (c // inner) % mid, c % inner
        z, x, k = step(z, x, k)
        route.append((c, (z % outer * mid + x % mid) * inner + k % inner))
    return route


def broadcast_band(tail, block, source):
    outer, mid, inner = COL_PARTS
    count = outer * mid * inner
    rows_total = tail.shape[0] + block.shape[0]
    if lax.axis_size("col") != count or mid != 4 or outer != 2 or inner != 2 or rows_total % 4 != 0:
        joined = jnp.concatenate([shifted(tail, "col", 1), block], axis=0)
        return spread(joined, "col", source)
    me = lax.axis_index("col")
    value = jnp.concatenate([tail, block], axis=0)
    split = tail.shape[0]
    half = rows_total // 2
    quarter = half // 2

    def deltas(origin):
        dz = (me // (mid * inner) - origin // (mid * inner)) % outer
        dx = ((me // inner) % mid - (origin // inner) % mid) % mid
        dk = (me % inner - origin % inner) % inner
        return dz, dx, dk

    tz, tx, tk = deltas((source + count - 1) % count)
    bz, bx, bk = deltas(source)
    core = me % inner
    start = core * half
    rows = start + lax.broadcasted_iota(jnp.int32, (half, 1), 0)

    def pick(tail_test, block_test):
        return jnp.where(rows < split, tail_test, block_test)

    flip = col_route(lambda z, x, k: (z, x, k + 1))
    wanted = lax.dynamic_slice_in_dim(value, (1 - core) * half, half)
    got = lax.ppermute(wanted, "col", flip)
    mine = jnp.where(pick(tk == 1, bk == 1), got, lax.dynamic_slice_in_dim(value, start, half))
    plus = col_route(lambda z, x, k: (z, x + 1, k))
    minus = col_route(lambda z, x, k: (z, x - 1, k))
    from_left = lax.ppermute(mine, "col", plus)
    from_right = lax.ppermute(mine, "col", minus)
    mine = jnp.where(pick(tx == 1, bx == 1), from_left, jnp.where(pick(tx == 3, bx == 3), from_right, mine))
    first = lax.ppermute(mine[:quarter], "col", plus)
    second = lax.ppermute(mine[quarter:], "col", minus)
    mine = jnp.where(pick(tx == 2, bx == 2), jnp.concatenate([first, second], axis=0), mine)
    got = lax.ppermute(mine, "col", col_route(lambda z, x, k: (z + 1, x, k)))
    mine = jnp.where(pick(tz == 1, bz == 1), got, mine)
    other = lax.ppermute(mine, "col", flip)
    return jnp.where(core == 0, jnp.concatenate([mine, other], axis=0), jnp.concatenate([other, mine], axis=0))


def broadcast_block(block, source):
    count = lax.axis_size("col")
    piece = block.shape[0] // count
    parts = block.reshape(count, piece, block.shape[1])
    got = lax.all_to_all(parts, "col", 0, 0, tiled=False)
    early = lax.dynamic_index_in_dim(got, (source + count - 1) % count, 0, keepdims=False)
    late = lax.dynamic_index_in_dim(got, source, 0, keepdims=False)
    pair = jnp.stack([early, late])[:, ::-1]
    spread_out = jnp.broadcast_to(pair[None], (count,) + pair.shape)
    return lax.all_to_all(spread_out, "col", 0, 0, tiled=False)


def power_int(frac, exps):
    square = frac * frac
    return jnp.where(
        exps == 0,
        jnp.ones_like(frac),
        jnp.where(exps == 1, frac, jnp.where(exps == 2, square, square * frac)),
    )


def cone_matrix(lengths, exps, lags):
    rows = lengths.shape[0]
    row_pos = lax.broadcasted_iota(jnp.int32, (rows, rows + lags - 1), 0)
    col_pos = lax.broadcasted_iota(jnp.int32, (rows, rows + lags - 1), 1)
    lag = row_pos + (lags - 1) - col_pos
    span = lengths[:, None]
    valid = (lag >= 0) & (lag < span)
    frac = (span.astype(jnp.float32) - lag.astype(jnp.float32)) / span.astype(jnp.float32)
    cone = jnp.where(valid, power_int(frac, exps[:, None]), jnp.zeros_like(frac))
    return cone / jnp.sum(cone, axis=1, keepdims=True)


def reversed_cone(lengths, exps, lags, depth):
    rows = lengths.shape[0]
    row_pos = lax.broadcasted_iota(jnp.int32, (rows, depth), 0)
    col_pos = lax.broadcasted_iota(jnp.int32, (rows, depth), 1)
    lag = row_pos + col_pos - (depth - lags) + 1
    span = lengths[:, None]
    valid = (lag >= 0) & (lag < span)
    frac = (span.astype(jnp.float32) - lag.astype(jnp.float32)) / span.astype(jnp.float32)
    cone = jnp.where(valid, power_int(frac, exps[:, None]), jnp.zeros_like(frac))
    return cone / jnp.sum(cone, axis=1, keepdims=True)


def lag_kernel(lags, r_ref, q_ref, cp_ref, csum_ref, w_ref, o_ref):
    count = r_ref.shape[0]
    tail_count = lags // r_ref.shape[2]
    rows = jnp.concatenate(
        [r_ref[count - 1 - s, 1] for s in range(count)] + [r_ref[count - 1 - s, 0] for s in range(tail_count)],
        axis=0,
    )
    wide = rows.astype(jnp.float32)
    square = wide * wide
    row_norm = jnp.sum(square, axis=1, keepdims=True)
    inner = lax.dot_general(
        rows, q_ref[...], (((1,), (1,)), ((), ())), preferred_element_type=jnp.float32
    )
    dist = row_norm + cp_ref[...] - 2.0 * inner
    width = dist.shape[1]
    depth = dist.shape[0]
    skew = pltpu.roll(dist, width - lags + 1, 1, stride=1, stride_axis=0)
    ones = jnp.ones((8, square.shape[1]), jnp.float32)
    norm_rows = lax.dot_general(
        ones, square, (((1,), (1,)), ((), ())), precision=lax.Precision.HIGHEST,
        preferred_element_type=jnp.float32,
    )
    row_sum = lax.dot_general(
        norm_rows, w_ref[...], (((1,), (1,)), ((), ())), precision=lax.Precision.HIGHEST,
        preferred_element_type=jnp.float32,
    )
    count, share, block = o_ref.shape[0], 64, o_ref.shape[2]
    share = block // count
    chunk = 128
    band = chunk + lags
    span = block + chunk
    for m in range(block // chunk):
        low = depth - band - chunk * m
        part = jnp.dot(
            w_ref[chunk * m : chunk * (m + 1), low : low + band],
            skew[low : low + band, low : low + span],
            precision=lax.Precision.HIGH,
            preferred_element_type=jnp.float32,
        )
        lined = pltpu.roll(part, span - (chunk - 1), 1, stride=1, stride_axis=0)
        for h in range(chunk // share):
            o_ref[(chunk * m) // share + h, 0:share, :] = lined[share * h : share * (h + 1), :block]
    extra = o_ref.shape[1] - share
    tail_rows = jnp.concatenate(
        [csum_ref[...], row_sum[0:1, :], jnp.zeros((extra - 2, block), jnp.float32)], axis=0
    )
    for k in range(count):
        o_ref[k, share:, :] = tail_rows


def lag_total(row_rev, col_pad, col_norm, col_sum, weights, count, lags):
    depth = weights.shape[1]
    width = col_pad.shape[0]
    block = weights.shape[0]
    share = block // count
    flops = 2 * depth * width * col_pad.shape[1] + 6 * 2 * block * (128 + lags) * (block + 128)
    return pl.pallas_call(
        functools.partial(lag_kernel, lags),
        out_shape=jax.ShapeDtypeStruct((count, share + 8, block), jnp.float32),
        in_specs=[pl.BlockSpec(memory_space=pltpu.VMEM)] * 5,
        out_specs=pl.BlockSpec(memory_space=pltpu.VMEM),
        cost_estimate=pl.CostEstimate(
            flops=flops, transcendentals=0, bytes_accessed=4 * (block * block + block * depth) + 2 * (depth + width) * 256
        ),
    )(row_rev, col_pad, col_norm, col_sum, weights)


def shards(snapshots, offsets, window_len, cone_exp):
    block = snapshots.shape[0]
    lags = LAGS
    count = lax.axis_size("col")
    tail = snapshots[block - (lags - 1) :]
    history = shifted(tail, "col", 1)
    col_ext = jnp.concatenate([history, snapshots], axis=0)
    chosen = lax.dynamic_index_in_dim(offsets, lax.axis_index("row"), 0, keepdims=False)
    pieces = broadcast_block(snapshots, chosen)
    row_begin = chosen * block
    col_begin = lax.axis_index("col") * block
    extent = block + lags
    row_lengths = lax.dynamic_slice_in_dim(window_len, row_begin, block)
    row_exps = lax.dynamic_slice_in_dim(cone_exp, row_begin, block)
    row_weights = reversed_cone(row_lengths, row_exps, lags, extent)
    col_weights = cone_matrix(
        lax.dynamic_slice_in_dim(window_len, col_begin, block),
        lax.dynamic_slice_in_dim(cone_exp, col_begin, block),
        lags,
    )
    col_wide = col_ext.astype(jnp.float32)
    col_part = jnp.sum(col_wide * col_wide, axis=1)
    width = 2 * block
    col_pad = jnp.pad(col_ext, ((0, width - col_ext.shape[0]), (0, 0)))
    col_part_pad = jnp.pad(col_part, (0, width - col_ext.shape[0]))
    col_sum = jnp.dot(col_weights, col_part, precision=lax.Precision.HIGHEST, preferred_element_type=jnp.float32)
    n_chan = lax.axis_size("chan")
    share = block // n_chan
    payload = lag_total(pieces, col_pad, col_part_pad[None, :], col_sum[None, :], row_weights, n_chan, lags)
    mine = jnp.sum(lax.all_to_all(payload, "chan", 0, 0, tiled=False), axis=0)
    row_sum = lax.dynamic_slice_in_dim(mine[share + 1], lax.axis_index("chan") * share, share)
    row_scale = jnp.sqrt(row_sum / C + epsilon)
    col_scale = jnp.sqrt(mine[share] / C + epsilon)
    return jnp.exp(-mine[:share] / (2.0 * C * row_scale[:, None] * col_scale[None, :]))


def solution(mesh):
    in_specs = (P("col", "chan"), P(), P(), P())
    out_specs = P(("row", "chan"), "col")
    return jax.shard_map(shards, mesh=mesh, in_specs=in_specs, out_specs=out_specs, check_vma=False)
```

```python
import functools

import jax
import jax.numpy as jnp
from jax import lax
from jax.experimental import pallas as pl
from jax.experimental.pallas import tpu as pltpu
from jax.sharding import PartitionSpec as P

C = 2048
LAGS = 256


epsilon = 1e-05


def shifted(block, axis, distance):
    devices = range(lax.axis_size(axis))
    route = [((i - distance) % len(devices), i) for i in devices]
    return lax.ppermute(block, axis, route)


def spread(value, axis, source):
    kept = jnp.where(lax.axis_index(axis) == source, value, 0).astype(value.dtype)
    return lax.psum(kept, axis)


COL_PARTS = (2, 4, 2)


def col_route(step):
    outer, mid, inner = COL_PARTS
    route = []
    for c in range(outer * mid * inner):
        z, x, k = c // (mid * inner), (c // inner) % mid, c % inner
        z, x, k = step(z, x, k)
        route.append((c, (z % outer * mid + x % mid) * inner + k % inner))
    return route


def broadcast_band(tail, block, source):
    outer, mid, inner = COL_PARTS
    count = outer * mid * inner
    rows_total = tail.shape[0] + block.shape[0]
    if lax.axis_size("col") != count or mid != 4 or outer != 2 or inner != 2 or rows_total % 4 != 0:
        joined = jnp.concatenate([shifted(tail, "col", 1), block], axis=0)
        return spread(joined, "col", source)
    me = lax.axis_index("col")
    value = jnp.concatenate([tail, block], axis=0)
    split = tail.shape[0]
    half = rows_total // 2
    quarter = half // 2

    def deltas(origin):
        dz = (me // (mid * inner) - origin // (mid * inner)) % outer
        dx = ((me // inner) % mid - (origin // inner) % mid) % mid
        dk = (me % inner - origin % inner) % inner
        return dz, dx, dk

    tz, tx, tk = deltas((source + count - 1) % count)
    bz, bx, bk = deltas(source)
    core = me % inner
    start = core * half
    rows = start + lax.broadcasted_iota(jnp.int32, (half, 1), 0)

    def pick(tail_test, block_test):
        return jnp.where(rows < split, tail_test, block_test)

    flip = col_route(lambda z, x, k: (z, x, k + 1))
    wanted = lax.dynamic_slice_in_dim(value, (1 - core) * half, half)
    got = lax.ppermute(wanted, "col", flip)
    mine = jnp.where(pick(tk == 1, bk == 1), got, lax.dynamic_slice_in_dim(value, start, half))
    plus = col_route(lambda z, x, k: (z, x + 1, k))
    minus = col_route(lambda z, x, k: (z, x - 1, k))
    from_left = lax.ppermute(mine, "col", plus)
    from_right = lax.ppermute(mine, "col", minus)
    mine = jnp.where(pick(tx == 1, bx == 1), from_left, jnp.where(pick(tx == 3, bx == 3), from_right, mine))
    first = lax.ppermute(mine[:quarter], "col", plus)
    second = lax.ppermute(mine[quarter:], "col", minus)
    mine = jnp.where(pick(tx == 2, bx == 2), jnp.concatenate([first, second], axis=0), mine)
    got = lax.ppermute(mine, "col", col_route(lambda z, x, k: (z + 1, x, k)))
    mine = jnp.where(pick(tz == 1, bz == 1), got, mine)
    other = lax.ppermute(mine, "col", flip)
    return jnp.where(core == 0, jnp.concatenate([mine, other], axis=0), jnp.concatenate([other, mine], axis=0))


def broadcast_block(block, source):
    count = lax.axis_size("col")
    piece = block.shape[0] // count
    parts = block.reshape(count, piece, block.shape[1])
    got = lax.all_to_all(parts, "col", 0, 0, tiled=False)
    early = lax.dynamic_index_in_dim(got, (source + count - 1) % count, 0, keepdims=False)
    late = lax.dynamic_index_in_dim(got, source, 0, keepdims=False)
    pair = jnp.stack([early, late])[:, ::-1]
    spread_out = jnp.broadcast_to(pair[None], (count,) + pair.shape)
    return lax.all_to_all(spread_out, "col", 0, 0, tiled=False)


def power_int(frac, exps):
    square = frac * frac
    return jnp.where(
        exps == 0,
        jnp.ones_like(frac),
        jnp.where(exps == 1, frac, jnp.where(exps == 2, square, square * frac)),
    )


def cone_matrix(lengths, exps, lags):
    rows = lengths.shape[0]
    row_pos = lax.broadcasted_iota(jnp.int32, (rows, rows + lags - 1), 0)
    col_pos = lax.broadcasted_iota(jnp.int32, (rows, rows + lags - 1), 1)
    lag = row_pos + (lags - 1) - col_pos
    span = lengths[:, None]
    valid = (lag >= 0) & (lag < span)
    frac = (span.astype(jnp.float32) - lag.astype(jnp.float32)) / span.astype(jnp.float32)
    cone = jnp.where(valid, power_int(frac, exps[:, None]), jnp.zeros_like(frac))
    return cone / jnp.sum(cone, axis=1, keepdims=True)


def reversed_cone(lengths, exps, lags, depth):
    rows = lengths.shape[0]
    row_pos = lax.broadcasted_iota(jnp.int32, (rows, depth), 0)
    col_pos = lax.broadcasted_iota(jnp.int32, (rows, depth), 1)
    lag = row_pos + col_pos - (depth - lags) + 1
    span = lengths[:, None]
    valid = (lag >= 0) & (lag < span)
    frac = (span.astype(jnp.float32) - lag.astype(jnp.float32)) / span.astype(jnp.float32)
    cone = jnp.where(valid, power_int(frac, exps[:, None]), jnp.zeros_like(frac))
    return cone / jnp.sum(cone, axis=1, keepdims=True)


def lag_kernel(lags, r_ref, q_ref, cp_ref, csum_ref, w_ref, o_ref):
    count = r_ref.shape[0]
    tail_count = lags // r_ref.shape[2]
    rows = jnp.concatenate(
        [r_ref[count - 1 - s, 1] for s in range(count)] + [r_ref[count - 1 - s, 0] for s in range(tail_count)],
        axis=0,
    )
    wide = rows.astype(jnp.float32)
    square = wide * wide
    row_norm = jnp.sum(square, axis=1, keepdims=True)
    inner = lax.dot_general(
        rows, q_ref[...], (((1,), (1,)), ((), ())), preferred_element_type=jnp.float32
    )
    depth = inner.shape[0]
    near = row_norm + cp_ref[...] - 2.0 * inner
    width = 2 * o_ref.shape[2]
    dist = jnp.concatenate([near, jnp.zeros((depth, width - near.shape[1]), jnp.float32)], axis=1)
    skew = pltpu.roll(dist, width - lags + 1, 1, stride=1, stride_axis=0)
    skew_hi = skew.astype(jnp.bfloat16)
    skew_lo = (skew - skew_hi.astype(jnp.float32)).astype(jnp.bfloat16)
    weights = w_ref[...]
    w_hi = weights.astype(jnp.bfloat16)
    w_lo = (weights - w_hi.astype(jnp.float32)).astype(jnp.bfloat16)
    ones = jnp.ones((8, square.shape[1]), jnp.float32)
    norm_rows = lax.dot_general(
        ones, square, (((1,), (1,)), ((), ())), precision=lax.Precision.HIGHEST,
        preferred_element_type=jnp.float32,
    )
    row_sum = lax.dot_general(
        norm_rows, w_ref[...], (((1,), (1,)), ((), ())), precision=lax.Precision.HIGHEST,
        preferred_element_type=jnp.float32,
    )
    count, share, block = o_ref.shape[0], 64, o_ref.shape[2]
    share = block // count
    chunk = 128
    band = chunk + lags
    span = block + chunk
    for m in range(block // chunk):
        low = depth - band - chunk * m
        rows_at = slice(chunk * m, chunk * (m + 1))
        cols_at = slice(low, low + band)
        out_at = slice(low, low + span)
        part = (
            jnp.dot(w_hi[rows_at, cols_at], skew_hi[cols_at, out_at], preferred_element_type=jnp.float32)
            + jnp.dot(w_hi[rows_at, cols_at], skew_lo[cols_at, out_at], preferred_element_type=jnp.float32)
            + jnp.dot(w_lo[rows_at, cols_at], skew_hi[cols_at, out_at], preferred_element_type=jnp.float32)
        )
        lined = pltpu.roll(part, span - (chunk - 1), 1, stride=1, stride_axis=0)
        for h in range(chunk // share):
            o_ref[(chunk * m) // share + h, 0:share, :] = lined[share * h : share * (h + 1), :block]
    extra = o_ref.shape[1] - share
    tail_rows = jnp.concatenate(
        [csum_ref[...], row_sum[0:1, :], jnp.zeros((extra - 2, block), jnp.float32)], axis=0
    )
    for k in range(count):
        o_ref[k, share:, :] = tail_rows


def lag_total(row_rev, col_pad, col_norm, col_sum, weights, count, lags):
    depth = weights.shape[1]
    width = col_pad.shape[0]
    block = weights.shape[0]
    share = block // count
    flops = 2 * depth * width * col_pad.shape[1] + 6 * 2 * block * (128 + lags) * (block + 128)
    return pl.pallas_call(
        functools.partial(lag_kernel, lags),
        out_shape=jax.ShapeDtypeStruct((count, share + 8, block), jnp.float32),
        in_specs=[pl.BlockSpec(memory_space=pltpu.VMEM)] * 5,
        out_specs=pl.BlockSpec(memory_space=pltpu.VMEM),
        cost_estimate=pl.CostEstimate(
            flops=flops, transcendentals=0, bytes_accessed=4 * (block * block + block * depth) + 2 * (depth + width) * 256
        ),
    )(row_rev, col_pad, col_norm, col_sum, weights)


def shards(snapshots, offsets, window_len, cone_exp):
    block = snapshots.shape[0]
    lags = LAGS
    count = lax.axis_size("col")
    tail = snapshots[block - (lags - 1) :]
    history = shifted(tail, "col", 1)
    col_ext = jnp.concatenate([history, snapshots], axis=0)
    chosen = lax.dynamic_index_in_dim(offsets, lax.axis_index("row"), 0, keepdims=False)
    pieces = broadcast_block(snapshots, chosen)
    row_begin = chosen * block
    col_begin = lax.axis_index("col") * block
    extent = block + lags
    row_lengths = lax.dynamic_slice_in_dim(window_len, row_begin, block)
    row_exps = lax.dynamic_slice_in_dim(cone_exp, row_begin, block)
    row_weights = reversed_cone(row_lengths, row_exps, lags, extent)
    col_weights = cone_matrix(
        lax.dynamic_slice_in_dim(window_len, col_begin, block),
        lax.dynamic_slice_in_dim(cone_exp, col_begin, block),
        lags,
    )
    col_wide = col_ext.astype(jnp.float32)
    col_part = jnp.sum(col_wide * col_wide, axis=1)
    extent_rows = block + lags
    col_pad = jnp.pad(col_ext, ((0, extent_rows - col_ext.shape[0]), (0, 0)))
    col_part_pad = jnp.pad(col_part, (0, extent_rows - col_ext.shape[0]))
    col_sum = jnp.sum(col_weights * col_part[None, :], axis=1)
    n_chan = lax.axis_size("chan")
    share = block // n_chan
    payload = lag_total(pieces, col_pad, col_part_pad[None, :], col_sum[None, :], row_weights, n_chan, lags)
    mine = jnp.sum(lax.all_to_all(payload, "chan", 0, 0, tiled=False), axis=0)
    row_sum = lax.dynamic_slice_in_dim(mine[share + 1], lax.axis_index("chan") * share, share)
    row_scale = jnp.sqrt(row_sum / C + epsilon)
    col_scale = jnp.sqrt(mine[share] / C + epsilon)
    return jnp.exp(-mine[:share] / (2.0 * C * row_scale[:, None] * col_scale[None, :]))


def solution(mesh):
    in_specs = (P("col", "chan"), P(), P(), P())
    out_specs = P(("row", "chan"), "col")
    return jax.shard_map(shards, mesh=mesh, in_specs=in_specs, out_specs=out_specs, check_vma=False)
```

```python
import functools

import jax
import jax.numpy as jnp
from jax import lax
from jax.experimental import pallas as pl
from jax.experimental.pallas import tpu as pltpu
from jax.sharding import PartitionSpec as P

C = 2048
LAGS = 256


epsilon = 1e-05


def shifted(block, axis, distance):
    devices = range(lax.axis_size(axis))
    route = [((i - distance) % len(devices), i) for i in devices]
    return lax.ppermute(block, axis, route)


def spread(value, axis, source):
    kept = jnp.where(lax.axis_index(axis) == source, value, 0).astype(value.dtype)
    return lax.psum(kept, axis)


COL_PARTS = (2, 4, 2)


def col_route(step):
    outer, mid, inner = COL_PARTS
    route = []
    for c in range(outer * mid * inner):
        z, x, k = c // (mid * inner), (c // inner) % mid, c % inner
        z, x, k = step(z, x, k)
        route.append((c, (z % outer * mid + x % mid) * inner + k % inner))
    return route


def broadcast_band(tail, block, source):
    outer, mid, inner = COL_PARTS
    count = outer * mid * inner
    rows_total = tail.shape[0] + block.shape[0]
    if lax.axis_size("col") != count or mid != 4 or outer != 2 or inner != 2 or rows_total % 4 != 0:
        joined = jnp.concatenate([shifted(tail, "col", 1), block], axis=0)
        return spread(joined, "col", source)
    me = lax.axis_index("col")
    value = jnp.concatenate([tail, block], axis=0)
    split = tail.shape[0]
    half = rows_total // 2
    quarter = half // 2

    def deltas(origin):
        dz = (me // (mid * inner) - origin // (mid * inner)) % outer
        dx = ((me // inner) % mid - (origin // inner) % mid) % mid
        dk = (me % inner - origin % inner) % inner
        return dz, dx, dk

    tz, tx, tk = deltas((source + count - 1) % count)
    bz, bx, bk = deltas(source)
    core = me % inner
    start = core * half
    rows = start + lax.broadcasted_iota(jnp.int32, (half, 1), 0)

    def pick(tail_test, block_test):
        return jnp.where(rows < split, tail_test, block_test)

    flip = col_route(lambda z, x, k: (z, x, k + 1))
    wanted = lax.dynamic_slice_in_dim(value, (1 - core) * half, half)
    got = lax.ppermute(wanted, "col", flip)
    mine = jnp.where(pick(tk == 1, bk == 1), got, lax.dynamic_slice_in_dim(value, start, half))
    plus = col_route(lambda z, x, k: (z, x + 1, k))
    minus = col_route(lambda z, x, k: (z, x - 1, k))
    from_left = lax.ppermute(mine, "col", plus)
    from_right = lax.ppermute(mine, "col", minus)
    mine = jnp.where(pick(tx == 1, bx == 1), from_left, jnp.where(pick(tx == 3, bx == 3), from_right, mine))
    first = lax.ppermute(mine[:quarter], "col", plus)
    second = lax.ppermute(mine[quarter:], "col", minus)
    mine = jnp.where(pick(tx == 2, bx == 2), jnp.concatenate([first, second], axis=0), mine)
    got = lax.ppermute(mine, "col", col_route(lambda z, x, k: (z + 1, x, k)))
    mine = jnp.where(pick(tz == 1, bz == 1), got, mine)
    other = lax.ppermute(mine, "col", flip)
    return jnp.where(core == 0, jnp.concatenate([mine, other], axis=0), jnp.concatenate([other, mine], axis=0))


def broadcast_block(block, source, held):
    count = lax.axis_size("col")
    piece = block.shape[0] // count
    parts = block.reshape(count, piece, block.shape[1])
    got = lax.all_to_all(parts, "col", 0, 0, tiled=False)
    got, held = lax.optimization_barrier((got, held))
    early = lax.dynamic_index_in_dim(got, (source + count - 1) % count, 0, keepdims=False)
    late = lax.dynamic_index_in_dim(got, source, 0, keepdims=False)
    pair = jnp.stack([early, late])[:, ::-1]
    spread_out = jnp.broadcast_to(pair[None], (count,) + pair.shape)
    return lax.all_to_all(spread_out, "col", 0, 0, tiled=False), held


def power_int(frac, exps):
    square = frac * frac
    return jnp.where(
        exps == 0,
        jnp.ones_like(frac),
        jnp.where(exps == 1, frac, jnp.where(exps == 2, square, square * frac)),
    )


def cone_matrix(lengths, exps, lags):
    rows = lengths.shape[0]
    row_pos = lax.broadcasted_iota(jnp.int32, (rows, rows + lags - 1), 0)
    col_pos = lax.broadcasted_iota(jnp.int32, (rows, rows + lags - 1), 1)
    lag = row_pos + (lags - 1) - col_pos
    span = lengths[:, None]
    valid = (lag >= 0) & (lag < span)
    frac = (span.astype(jnp.float32) - lag.astype(jnp.float32)) / span.astype(jnp.float32)
    cone = jnp.where(valid, power_int(frac, exps[:, None]), jnp.zeros_like(frac))
    return cone / jnp.sum(cone, axis=1, keepdims=True)


def reversed_cone(lengths, exps, lags, depth):
    rows = lengths.shape[0]
    row_pos = lax.broadcasted_iota(jnp.int32, (rows, depth), 0)
    col_pos = lax.broadcasted_iota(jnp.int32, (rows, depth), 1)
    lag = row_pos + col_pos - (depth - lags) + 1
    span = lengths[:, None]
    valid = (lag >= 0) & (lag < span)
    frac = (span.astype(jnp.float32) - lag.astype(jnp.float32)) / span.astype(jnp.float32)
    cone = jnp.where(valid, power_int(frac, exps[:, None]), jnp.zeros_like(frac))
    return cone / jnp.sum(cone, axis=1, keepdims=True)


def lag_kernel(lags, r_ref, q_ref, cp_ref, csum_ref, w_ref, o_ref):
    count = r_ref.shape[0]
    tail_count = lags // r_ref.shape[2]
    rows = jnp.concatenate(
        [r_ref[count - 1 - s, 1] for s in range(count)] + [r_ref[count - 1 - s, 0] for s in range(tail_count)],
        axis=0,
    )
    wide = rows.astype(jnp.float32)
    square = wide * wide
    row_norm = jnp.sum(square, axis=1, keepdims=True)
    inner = lax.dot_general(
        rows, q_ref[...], (((1,), (1,)), ((), ())), preferred_element_type=jnp.float32
    )
    depth = inner.shape[0]
    near = row_norm + cp_ref[...] - 2.0 * inner
    width = 2 * o_ref.shape[2]
    dist = jnp.concatenate([near, jnp.zeros((depth, width - near.shape[1]), jnp.float32)], axis=1)
    skew = pltpu.roll(dist, width - lags + 1, 1, stride=1, stride_axis=0)
    skew_hi = skew.astype(jnp.bfloat16)
    skew_lo = (skew - skew_hi.astype(jnp.float32)).astype(jnp.bfloat16)
    weights = w_ref[...]
    w_hi = weights.astype(jnp.bfloat16)
    w_lo = (weights - w_hi.astype(jnp.float32)).astype(jnp.bfloat16)
    ones = jnp.ones((8, square.shape[1]), jnp.float32)
    norm_rows = lax.dot_general(
        ones, square, (((1,), (1,)), ((), ())), precision=lax.Precision.HIGHEST,
        preferred_element_type=jnp.float32,
    )
    row_sum = lax.dot_general(
        norm_rows, w_ref[...], (((1,), (1,)), ((), ())), precision=lax.Precision.HIGHEST,
        preferred_element_type=jnp.float32,
    )
    count, share, block = o_ref.shape[0], 64, o_ref.shape[2]
    share = block // count
    chunk = 128
    band = chunk + lags
    span = block + chunk
    for m in range(block // chunk):
        low = depth - band - chunk * m
        rows_at = slice(chunk * m, chunk * (m + 1))
        cols_at = slice(low, low + band)
        out_at = slice(low, low + span)
        part = (
            jnp.dot(w_hi[rows_at, cols_at], skew_hi[cols_at, out_at], preferred_element_type=jnp.float32)
            + jnp.dot(w_hi[rows_at, cols_at], skew_lo[cols_at, out_at], preferred_element_type=jnp.float32)
            + jnp.dot(w_lo[rows_at, cols_at], skew_hi[cols_at, out_at], preferred_element_type=jnp.float32)
        )
        lined = pltpu.roll(part, span - (chunk - 1), 1, stride=1, stride_axis=0)
        for h in range(chunk // share):
            o_ref[(chunk * m) // share + h, 0:share, :] = lined[share * h : share * (h + 1), :block]
    extra = o_ref.shape[1] - share
    tail_rows = jnp.concatenate(
        [csum_ref[...], row_sum[0:1, :], jnp.zeros((extra - 2, block), jnp.float32)], axis=0
    )
    for k in range(count):
        o_ref[k, share:, :] = tail_rows


def lag_total(row_rev, col_pad, col_norm, col_sum, weights, count, lags):
    depth = weights.shape[1]
    width = col_pad.shape[0]
    block = weights.shape[0]
    share = block // count
    flops = 2 * depth * width * col_pad.shape[1] + 6 * 2 * block * (128 + lags) * (block + 128)
    return pl.pallas_call(
        functools.partial(lag_kernel, lags),
        out_shape=jax.ShapeDtypeStruct((count, share + 8, block), jnp.float32),
        in_specs=[pl.BlockSpec(memory_space=pltpu.VMEM)] * 5,
        out_specs=pl.BlockSpec(memory_space=pltpu.VMEM),
        cost_estimate=pl.CostEstimate(
            flops=flops, transcendentals=0, bytes_accessed=4 * (block * block + block * depth) + 2 * (depth + width) * 256
        ),
    )(row_rev, col_pad, col_norm, col_sum, weights)


def shards(snapshots, offsets, window_len, cone_exp):
    block = snapshots.shape[0]
    lags = LAGS
    count = lax.axis_size("col")
    tail = snapshots[block - (lags - 1) :]
    history = shifted(tail, "col", 1)
    col_ext = jnp.concatenate([history, snapshots], axis=0)
    chosen = lax.dynamic_index_in_dim(offsets, lax.axis_index("row"), 0, keepdims=False)
    row_begin = chosen * block
    col_begin = lax.axis_index("col") * block
    extent = block + lags
    pieces, (row_lengths, row_exps) = broadcast_block(
        snapshots,
        chosen,
        (lax.dynamic_slice_in_dim(window_len, row_begin, block), lax.dynamic_slice_in_dim(cone_exp, row_begin, block)),
    )
    row_weights = reversed_cone(row_lengths, row_exps, lags, extent)
    col_weights = cone_matrix(
        lax.dynamic_slice_in_dim(window_len, col_begin, block),
        lax.dynamic_slice_in_dim(cone_exp, col_begin, block),
        lags,
    )
    col_wide = col_ext.astype(jnp.float32)
    col_part = jnp.sum(col_wide * col_wide, axis=1)
    extent_rows = block + lags
    col_pad = jnp.pad(col_ext, ((0, extent_rows - col_ext.shape[0]), (0, 0)))
    col_part_pad = jnp.pad(col_part, (0, extent_rows - col_ext.shape[0]))
    col_sum = jnp.sum(col_weights * col_part[None, :], axis=1)
    n_chan = lax.axis_size("chan")
    share = block // n_chan
    payload = lag_total(pieces, col_pad, col_part_pad[None, :], col_sum[None, :], row_weights, n_chan, lags)
    mine = jnp.sum(lax.all_to_all(payload, "chan", 0, 0, tiled=False), axis=0)
    row_sum = lax.dynamic_slice_in_dim(mine[share + 1], lax.axis_index("chan") * share, share)
    row_scale = jnp.sqrt(row_sum / C + epsilon)
    col_scale = jnp.sqrt(mine[share] / C + epsilon)
    return jnp.exp(-mine[:share] / (2.0 * C * row_scale[:, None] * col_scale[None, :]))


def solution(mesh):
    in_specs = (P("col", "chan"), P(), P(), P())
    out_specs = P(("row", "chan"), "col")
    return jax.shard_map(shards, mesh=mesh, in_specs=in_specs, out_specs=out_specs, check_vma=False)
```

```python
import functools

import jax
import jax.numpy as jnp
from jax import lax
from jax.experimental import pallas as pl
from jax.experimental.pallas import tpu as pltpu
from jax.sharding import PartitionSpec as P

C = 2048
LAGS = 256


epsilon = 1e-05


def shifted(block, axis, distance):
    devices = range(lax.axis_size(axis))
    route = [((i - distance) % len(devices), i) for i in devices]
    return lax.ppermute(block, axis, route)


def spread(value, axis, source):
    kept = jnp.where(lax.axis_index(axis) == source, value, 0).astype(value.dtype)
    return lax.psum(kept, axis)


COL_PARTS = (2, 4, 2)


def col_route(step):
    outer, mid, inner = COL_PARTS
    route = []
    for c in range(outer * mid * inner):
        z, x, k = c // (mid * inner), (c // inner) % mid, c % inner
        z, x, k = step(z, x, k)
        route.append((c, (z % outer * mid + x % mid) * inner + k % inner))
    return route


def broadcast_band(tail, block, source):
    outer, mid, inner = COL_PARTS
    count = outer * mid * inner
    rows_total = tail.shape[0] + block.shape[0]
    if lax.axis_size("col") != count or mid != 4 or outer != 2 or inner != 2 or rows_total % 4 != 0:
        joined = jnp.concatenate([shifted(tail, "col", 1), block], axis=0)
        return spread(joined, "col", source)
    me = lax.axis_index("col")
    value = jnp.concatenate([tail, block], axis=0)
    split = tail.shape[0]
    half = rows_total // 2
    quarter = half // 2

    def deltas(origin):
        dz = (me // (mid * inner) - origin // (mid * inner)) % outer
        dx = ((me // inner) % mid - (origin // inner) % mid) % mid
        dk = (me % inner - origin % inner) % inner
        return dz, dx, dk

    tz, tx, tk = deltas((source + count - 1) % count)
    bz, bx, bk = deltas(source)
    core = me % inner
    start = core * half
    rows = start + lax.broadcasted_iota(jnp.int32, (half, 1), 0)

    def pick(tail_test, block_test):
        return jnp.where(rows < split, tail_test, block_test)

    flip = col_route(lambda z, x, k: (z, x, k + 1))
    wanted = lax.dynamic_slice_in_dim(value, (1 - core) * half, half)
    got = lax.ppermute(wanted, "col", flip)
    mine = jnp.where(pick(tk == 1, bk == 1), got, lax.dynamic_slice_in_dim(value, start, half))
    plus = col_route(lambda z, x, k: (z, x + 1, k))
    minus = col_route(lambda z, x, k: (z, x - 1, k))
    from_left = lax.ppermute(mine, "col", plus)
    from_right = lax.ppermute(mine, "col", minus)
    mine = jnp.where(pick(tx == 1, bx == 1), from_left, jnp.where(pick(tx == 3, bx == 3), from_right, mine))
    first = lax.ppermute(mine[:quarter], "col", plus)
    second = lax.ppermute(mine[quarter:], "col", minus)
    mine = jnp.where(pick(tx == 2, bx == 2), jnp.concatenate([first, second], axis=0), mine)
    got = lax.ppermute(mine, "col", col_route(lambda z, x, k: (z + 1, x, k)))
    mine = jnp.where(pick(tz == 1, bz == 1), got, mine)
    other = lax.ppermute(mine, "col", flip)
    return jnp.where(core == 0, jnp.concatenate([mine, other], axis=0), jnp.concatenate([other, mine], axis=0))


def broadcast_block(block, source):
    count = lax.axis_size("col")
    piece = block.shape[0] // count
    parts = block.reshape(count, piece, block.shape[1])
    got = lax.all_to_all(parts, "col", 0, 0, tiled=False)
    early = lax.dynamic_index_in_dim(got, lax.rem(source + count - 1, count), 0, keepdims=False)
    late = lax.dynamic_index_in_dim(got, source, 0, keepdims=False)
    pair = jnp.stack([early, late])[:, ::-1]
    spread_out = jnp.broadcast_to(pair[None], (count,) + pair.shape)
    return lax.all_to_all(spread_out, "col", 0, 0, tiled=False)


def power_int(frac, exps):
    square = frac * frac
    return jnp.where(
        exps == 0,
        jnp.ones_like(frac),
        jnp.where(exps == 1, frac, jnp.where(exps == 2, square, square * frac)),
    )


def cone_matrix(lengths, exps, lags):
    rows = lengths.shape[0]
    row_pos = lax.broadcasted_iota(jnp.int32, (rows, rows + lags - 1), 0)
    col_pos = lax.broadcasted_iota(jnp.int32, (rows, rows + lags - 1), 1)
    lag = row_pos + (lags - 1) - col_pos
    span = lengths[:, None]
    valid = (lag >= 0) & (lag < span)
    frac = (span.astype(jnp.float32) - lag.astype(jnp.float32)) / span.astype(jnp.float32)
    cone = jnp.where(valid, power_int(frac, exps[:, None]), jnp.zeros_like(frac))
    return cone / jnp.sum(cone, axis=1, keepdims=True)


def reversed_cone(lengths, exps, lags, depth):
    rows = lengths.shape[0]
    row_pos = lax.broadcasted_iota(jnp.int32, (rows, depth), 0)
    col_pos = lax.broadcasted_iota(jnp.int32, (rows, depth), 1)
    lag = row_pos + col_pos - (depth - lags) + 1
    span = lengths[:, None]
    valid = (lag >= 0) & (lag < span)
    frac = (span.astype(jnp.float32) - lag.astype(jnp.float32)) / span.astype(jnp.float32)
    cone = jnp.where(valid, power_int(frac, exps[:, None]), jnp.zeros_like(frac))
    return cone / jnp.sum(cone, axis=1, keepdims=True)


def lag_kernel(lags, r_ref, q_ref, cp_ref, csum_ref, w_ref, o_ref):
    count = r_ref.shape[0]
    tail_count = lags // r_ref.shape[2]
    rows = jnp.concatenate(
        [r_ref[count - 1 - s, 1] for s in range(count)] + [r_ref[count - 1 - s, 0] for s in range(tail_count)],
        axis=0,
    )
    wide = rows.astype(jnp.float32)
    square = wide * wide
    row_norm = jnp.sum(square, axis=1, keepdims=True)
    inner = lax.dot_general(
        rows, q_ref[...], (((1,), (1,)), ((), ())), preferred_element_type=jnp.float32
    )
    depth = inner.shape[0]
    near = row_norm + cp_ref[...] - 2.0 * inner
    width = 2 * o_ref.shape[2]
    dist = jnp.concatenate([near, jnp.zeros((depth, width - near.shape[1]), jnp.float32)], axis=1)
    skew = pltpu.roll(dist, width - lags, 1, stride=1, stride_axis=0)
    skew_hi = skew.astype(jnp.bfloat16)
    skew_lo = (skew - skew_hi.astype(jnp.float32)).astype(jnp.bfloat16)
    weights = w_ref[...]
    w_hi = weights.astype(jnp.bfloat16)
    w_lo = (weights - w_hi.astype(jnp.float32)).astype(jnp.bfloat16)
    ones = jnp.ones((8, square.shape[1]), jnp.float32)
    norm_rows = lax.dot_general(
        ones, square, (((1,), (1,)), ((), ())), precision=lax.Precision.HIGHEST,
        preferred_element_type=jnp.float32,
    )
    row_sum = lax.dot_general(
        norm_rows, w_ref[...], (((1,), (1,)), ((), ())), precision=lax.Precision.HIGHEST,
        preferred_element_type=jnp.float32,
    )
    count, share, block = o_ref.shape[0], 64, o_ref.shape[2]
    share = block // count
    chunk = 128
    band = chunk + lags
    span = block + chunk
    for m in range(block // chunk):
        low = depth - band - chunk * m
        rows_at = slice(chunk * m, chunk * (m + 1))
        cols_at = slice(low, low + band)
        out_at = slice(low, low + span)
        part = (
            jnp.dot(w_hi[rows_at, cols_at], skew_hi[cols_at, out_at], preferred_element_type=jnp.float32)
            + jnp.dot(w_hi[rows_at, cols_at], skew_lo[cols_at, out_at], preferred_element_type=jnp.float32)
            + jnp.dot(w_lo[rows_at, cols_at], skew_hi[cols_at, out_at], preferred_element_type=jnp.float32)
        )
        lined = pltpu.roll(part, span - (chunk - 1), 1, stride=1, stride_axis=0)
        for h in range(chunk // share):
            o_ref[(chunk * m) // share + h, 0:share, :] = lined[share * h : share * (h + 1), :block]
    extra = o_ref.shape[1] - share
    tail_rows = jnp.concatenate(
        [csum_ref[...], row_sum[0:1, :], jnp.zeros((extra - 2, block), jnp.float32)], axis=0
    )
    for k in range(count):
        o_ref[k, share:, :] = tail_rows


def lag_total(row_rev, col_pad, col_norm, col_sum, weights, count, lags):
    depth = weights.shape[1]
    width = col_pad.shape[0]
    block = weights.shape[0]
    share = block // count
    flops = 2 * depth * width * col_pad.shape[1] + 6 * 2 * block * (128 + lags) * (block + 128)
    return pl.pallas_call(
        functools.partial(lag_kernel, lags),
        out_shape=jax.ShapeDtypeStruct((count, share + 8, block), jnp.float32),
        in_specs=[pl.BlockSpec(memory_space=pltpu.VMEM)] * 5,
        out_specs=pl.BlockSpec(memory_space=pltpu.VMEM),
        cost_estimate=pl.CostEstimate(
            flops=flops, transcendentals=0, bytes_accessed=4 * (block * block + block * depth) + 2 * (depth + width) * 256
        ),
    )(row_rev, col_pad, col_norm, col_sum, weights)


def shards(snapshots, offsets, window_len, cone_exp):
    block = snapshots.shape[0]
    lags = LAGS
    tail = snapshots[block - lags :]
    history = shifted(tail, "col", 1)
    col_ext = jnp.concatenate([history, snapshots], axis=0)
    chosen = lax.dynamic_index_in_dim(offsets, lax.axis_index("row"), 0, keepdims=False)
    pieces = broadcast_block(snapshots, chosen)
    row_begin = chosen * block
    col_begin = lax.axis_index("col") * block
    extent = block + lags
    row_lengths = lax.dynamic_slice_in_dim(window_len, row_begin, block)
    row_exps = lax.dynamic_slice_in_dim(cone_exp, row_begin, block)
    row_weights = reversed_cone(row_lengths, row_exps, lags, extent)
    col_weights = cone_matrix(
        lax.dynamic_slice_in_dim(window_len, col_begin, block),
        lax.dynamic_slice_in_dim(cone_exp, col_begin, block),
        lags + 1,
    )
    col_wide = col_ext.astype(jnp.float32)
    col_part = jnp.sum(col_wide * col_wide, axis=1)
    col_sum = jnp.sum(col_weights * col_part[None, :], axis=1)
    n_chan = lax.axis_size("chan")
    share = block // n_chan
    payload = lag_total(pieces, col_ext, col_part[None, :], col_sum[None, :], row_weights, n_chan, lags)
    mine = jnp.sum(lax.all_to_all(payload, "chan", 0, 0, tiled=False), axis=0)
    row_sum = lax.dynamic_slice_in_dim(mine[share + 1], lax.axis_index("chan") * share, share)
    row_scale = jnp.sqrt(row_sum / C + epsilon)
    col_scale = jnp.sqrt(mine[share] / C + epsilon)
    return jnp.exp(-mine[:share] / (2.0 * C * row_scale[:, None] * col_scale[None, :]))


def solution(mesh):
    in_specs = (P("col", "chan"), P(), P(), P())
    out_specs = P(("row", "chan"), "col")
    return jax.shard_map(shards, mesh=mesh, in_specs=in_specs, out_specs=out_specs, check_vma=False)
```

```python
import functools

import jax
import jax.numpy as jnp
from jax import lax
from jax.experimental import pallas as pl
from jax.experimental.pallas import tpu as pltpu
from jax.sharding import PartitionSpec as P

C = 2048
LAGS = 256


epsilon = 1e-05


def shifted(block, axis, distance):
    devices = range(lax.axis_size(axis))
    route = [((i - distance) % len(devices), i) for i in devices]
    return lax.ppermute(block, axis, route)


def spread(value, axis, source):
    kept = jnp.where(lax.axis_index(axis) == source, value, 0).astype(value.dtype)
    return lax.psum(kept, axis)


COL_PARTS = (2, 4, 2)


def col_route(step):
    outer, mid, inner = COL_PARTS
    route = []
    for c in range(outer * mid * inner):
        z, x, k = c // (mid * inner), (c // inner) % mid, c % inner
        z, x, k = step(z, x, k)
        route.append((c, (z % outer * mid + x % mid) * inner + k % inner))
    return route


def broadcast_band(tail, block, source):
    outer, mid, inner = COL_PARTS
    count = outer * mid * inner
    rows_total = tail.shape[0] + block.shape[0]
    if lax.axis_size("col") != count or mid != 4 or outer != 2 or inner != 2 or rows_total % 4 != 0:
        joined = jnp.concatenate([shifted(tail, "col", 1), block], axis=0)
        return spread(joined, "col", source)
    me = lax.axis_index("col")
    value = jnp.concatenate([tail, block], axis=0)
    split = tail.shape[0]
    half = rows_total // 2
    quarter = half // 2

    def deltas(origin):
        dz = (me // (mid * inner) - origin // (mid * inner)) % outer
        dx = ((me // inner) % mid - (origin // inner) % mid) % mid
        dk = (me % inner - origin % inner) % inner
        return dz, dx, dk

    tz, tx, tk = deltas((source + count - 1) % count)
    bz, bx, bk = deltas(source)
    core = me % inner
    start = core * half
    rows = start + lax.broadcasted_iota(jnp.int32, (half, 1), 0)

    def pick(tail_test, block_test):
        return jnp.where(rows < split, tail_test, block_test)

    flip = col_route(lambda z, x, k: (z, x, k + 1))
    wanted = lax.dynamic_slice_in_dim(value, (1 - core) * half, half)
    got = lax.ppermute(wanted, "col", flip)
    mine = jnp.where(pick(tk == 1, bk == 1), got, lax.dynamic_slice_in_dim(value, start, half))
    plus = col_route(lambda z, x, k: (z, x + 1, k))
    minus = col_route(lambda z, x, k: (z, x - 1, k))
    from_left = lax.ppermute(mine, "col", plus)
    from_right = lax.ppermute(mine, "col", minus)
    mine = jnp.where(pick(tx == 1, bx == 1), from_left, jnp.where(pick(tx == 3, bx == 3), from_right, mine))
    first = lax.ppermute(mine[:quarter], "col", plus)
    second = lax.ppermute(mine[quarter:], "col", minus)
    mine = jnp.where(pick(tx == 2, bx == 2), jnp.concatenate([first, second], axis=0), mine)
    got = lax.ppermute(mine, "col", col_route(lambda z, x, k: (z + 1, x, k)))
    mine = jnp.where(pick(tz == 1, bz == 1), got, mine)
    other = lax.ppermute(mine, "col", flip)
    return jnp.where(core == 0, jnp.concatenate([mine, other], axis=0), jnp.concatenate([other, mine], axis=0))


def pick(stack, index):
    mask = lax.broadcasted_iota(jnp.int32, (stack.shape[0],) + (1,) * (stack.ndim - 1), 0) == index
    return jnp.sum(jnp.where(mask, stack, jnp.zeros_like(stack)), axis=0)


def broadcast_block(block, source):
    count = lax.axis_size("col")
    piece = block.shape[0] // count
    parts = block.reshape(count, piece, block.shape[1])
    got = lax.all_to_all(parts, "col", 0, 0, tiled=False)
    early = pick(got, lax.rem(source + count - 1, count))
    late = pick(got, source)
    pair = jnp.stack([early, late])[:, ::-1]
    spread_out = jnp.broadcast_to(pair[None], (count,) + pair.shape)
    return lax.all_to_all(spread_out, "col", 0, 0, tiled=False)


def power_int(frac, exps):
    square = frac * frac
    return jnp.where(
        exps == 0,
        jnp.ones_like(frac),
        jnp.where(exps == 1, frac, jnp.where(exps == 2, square, square * frac)),
    )


def cone_matrix(lengths, exps, lags):
    rows = lengths.shape[0]
    row_pos = lax.broadcasted_iota(jnp.int32, (rows, rows + lags - 1), 0)
    col_pos = lax.broadcasted_iota(jnp.int32, (rows, rows + lags - 1), 1)
    lag = row_pos + (lags - 1) - col_pos
    span = lengths[:, None]
    valid = (lag >= 0) & (lag < span)
    frac = (span.astype(jnp.float32) - lag.astype(jnp.float32)) / span.astype(jnp.float32)
    cone = jnp.where(valid, power_int(frac, exps[:, None]), jnp.zeros_like(frac))
    return cone / jnp.sum(cone, axis=1, keepdims=True)


def reversed_cone(lengths, exps, lags, depth):
    rows = lengths.shape[0]
    row_pos = lax.broadcasted_iota(jnp.int32, (rows, depth), 0)
    col_pos = lax.broadcasted_iota(jnp.int32, (rows, depth), 1)
    lag = row_pos + col_pos - (depth - lags) + 1
    span = lengths[:, None]
    valid = (lag >= 0) & (lag < span)
    frac = (span.astype(jnp.float32) - lag.astype(jnp.float32)) / span.astype(jnp.float32)
    cone = jnp.where(valid, power_int(frac, exps[:, None]), jnp.zeros_like(frac))
    return cone / jnp.sum(cone, axis=1, keepdims=True)


def lag_kernel(lags, r_ref, q_ref, cp_ref, csum_ref, w_ref, o_ref):
    count = r_ref.shape[0]
    tail_count = lags // r_ref.shape[2]
    rows = jnp.concatenate(
        [r_ref[count - 1 - s, 1] for s in range(count)] + [r_ref[count - 1 - s, 0] for s in range(tail_count)],
        axis=0,
    )
    wide = rows.astype(jnp.float32)
    square = wide * wide
    row_norm = jnp.sum(square, axis=1, keepdims=True)
    inner = lax.dot_general(
        rows, q_ref[...], (((1,), (1,)), ((), ())), preferred_element_type=jnp.float32
    )
    depth = inner.shape[0]
    near = row_norm + cp_ref[...] - 2.0 * inner
    width = 2 * o_ref.shape[2]
    dist = jnp.concatenate([near, jnp.zeros((depth, width - near.shape[1]), jnp.float32)], axis=1)
    skew = pltpu.roll(dist, width - lags, 1, stride=1, stride_axis=0)
    skew_hi = skew.astype(jnp.bfloat16)
    skew_lo = (skew - skew_hi.astype(jnp.float32)).astype(jnp.bfloat16)
    weights = w_ref[...]
    w_hi = weights.astype(jnp.bfloat16)
    w_lo = (weights - w_hi.astype(jnp.float32)).astype(jnp.bfloat16)
    ones = jnp.ones((8, square.shape[1]), jnp.float32)
    norm_rows = lax.dot_general(
        ones, square, (((1,), (1,)), ((), ())), precision=lax.Precision.HIGHEST,
        preferred_element_type=jnp.float32,
    )
    row_sum = lax.dot_general(
        norm_rows, w_ref[...], (((1,), (1,)), ((), ())), precision=lax.Precision.HIGHEST,
        preferred_element_type=jnp.float32,
    )
    count, share, block = o_ref.shape[0], 64, o_ref.shape[2]
    share = block // count
    chunk = 128
    band = chunk + lags
    span = block + chunk
    for m in range(block // chunk):
        low = depth - band - chunk * m
        rows_at = slice(chunk * m, chunk * (m + 1))
        cols_at = slice(low, low + band)
        out_at = slice(low, low + span)
        part = (
            jnp.dot(w_hi[rows_at, cols_at], skew_hi[cols_at, out_at], preferred_element_type=jnp.float32)
            + jnp.dot(w_hi[rows_at, cols_at], skew_lo[cols_at, out_at], preferred_element_type=jnp.float32)
            + jnp.dot(w_lo[rows_at, cols_at], skew_hi[cols_at, out_at], preferred_element_type=jnp.float32)
        )
        lined = pltpu.roll(part, span - (chunk - 1), 1, stride=1, stride_axis=0)
        for h in range(chunk // share):
            o_ref[(chunk * m) // share + h, 0:share, :] = lined[share * h : share * (h + 1), :block]
    extra = o_ref.shape[1] - share
    tail_rows = jnp.concatenate(
        [csum_ref[...], row_sum[0:1, :], jnp.zeros((extra - 2, block), jnp.float32)], axis=0
    )
    for k in range(count):
        o_ref[k, share:, :] = tail_rows


def lag_total(row_rev, col_pad, col_norm, col_sum, weights, count, lags):
    depth = weights.shape[1]
    width = col_pad.shape[0]
    block = weights.shape[0]
    share = block // count
    flops = 2 * depth * width * col_pad.shape[1] + 6 * 2 * block * (128 + lags) * (block + 128)
    return pl.pallas_call(
        functools.partial(lag_kernel, lags),
        out_shape=jax.ShapeDtypeStruct((count, share + 8, block), jnp.float32),
        in_specs=[pl.BlockSpec(memory_space=pltpu.VMEM)] * 5,
        out_specs=pl.BlockSpec(memory_space=pltpu.VMEM),
        cost_estimate=pl.CostEstimate(
            flops=flops, transcendentals=0, bytes_accessed=4 * (block * block + block * depth) + 2 * (depth + width) * 256
        ),
    )(row_rev, col_pad, col_norm, col_sum, weights)


def shards(snapshots, offsets, window_len, cone_exp):
    block = snapshots.shape[0]
    lags = LAGS
    tail = snapshots[block - lags :]
    history = shifted(tail, "col", 1)
    col_ext = jnp.concatenate([history, snapshots], axis=0)
    chosen = pick(offsets, lax.axis_index("row"))
    pieces = broadcast_block(snapshots, chosen)
    me = lax.axis_index("col")
    extent = block + lags
    lengths = window_len.reshape(-1, block)
    exps = cone_exp.reshape(-1, block)
    row_weights = reversed_cone(pick(lengths, chosen), pick(exps, chosen), lags, extent)
    col_weights = cone_matrix(pick(lengths, me), pick(exps, me), lags + 1)
    col_wide = col_ext.astype(jnp.float32)
    col_part = jnp.sum(col_wide * col_wide, axis=1)
    col_sum = jnp.sum(col_weights * col_part[None, :], axis=1)
    n_chan = lax.axis_size("chan")
    share = block // n_chan
    payload = lag_total(pieces, col_ext, col_part[None, :], col_sum[None, :], row_weights, n_chan, lags)
    mine = jnp.sum(lax.all_to_all(payload, "chan", 0, 0, tiled=False), axis=0)
    row_sum = lax.dynamic_slice_in_dim(mine[share + 1], lax.axis_index("chan") * share, share)
    row_scale = jnp.sqrt(row_sum / C + epsilon)
    col_scale = jnp.sqrt(mine[share] / C + epsilon)
    return jnp.exp(-mine[:share] / (2.0 * C * row_scale[:, None] * col_scale[None, :]))


def solution(mesh):
    in_specs = (P("col", "chan"), P(), P(), P())
    out_specs = P(("row", "chan"), "col")
    return jax.shard_map(shards, mesh=mesh, in_specs=in_specs, out_specs=out_specs, check_vma=False)
```

```python
import functools

import jax
import jax.numpy as jnp
from jax import lax
from jax.experimental import pallas as pl
from jax.experimental.pallas import tpu as pltpu
from jax.sharding import PartitionSpec as P

C = 2048
LAGS = 256


epsilon = 1e-05


def shifted(block, axis, distance):
    devices = range(lax.axis_size(axis))
    route = [((i - distance) % len(devices), i) for i in devices]
    return lax.ppermute(block, axis, route)


def spread(value, axis, source):
    kept = jnp.where(lax.axis_index(axis) == source, value, 0).astype(value.dtype)
    return lax.psum(kept, axis)


COL_PARTS = (2, 4, 2)


def col_route(step):
    outer, mid, inner = COL_PARTS
    route = []
    for c in range(outer * mid * inner):
        z, x, k = c // (mid * inner), (c // inner) % mid, c % inner
        z, x, k = step(z, x, k)
        route.append((c, (z % outer * mid + x % mid) * inner + k % inner))
    return route


def broadcast_band(tail, block, source):
    outer, mid, inner = COL_PARTS
    count = outer * mid * inner
    rows_total = tail.shape[0] + block.shape[0]
    if lax.axis_size("col") != count or mid != 4 or outer != 2 or inner != 2 or rows_total % 4 != 0:
        joined = jnp.concatenate([shifted(tail, "col", 1), block], axis=0)
        return spread(joined, "col", source)
    me = lax.axis_index("col")
    value = jnp.concatenate([tail, block], axis=0)
    split = tail.shape[0]
    half = rows_total // 2
    quarter = half // 2

    def deltas(origin):
        dz = (me // (mid * inner) - origin // (mid * inner)) % outer
        dx = ((me // inner) % mid - (origin // inner) % mid) % mid
        dk = (me % inner - origin % inner) % inner
        return dz, dx, dk

    tz, tx, tk = deltas((source + count - 1) % count)
    bz, bx, bk = deltas(source)
    core = me % inner
    start = core * half
    rows = start + lax.broadcasted_iota(jnp.int32, (half, 1), 0)

    def pick(tail_test, block_test):
        return jnp.where(rows < split, tail_test, block_test)

    flip = col_route(lambda z, x, k: (z, x, k + 1))
    wanted = lax.dynamic_slice_in_dim(value, (1 - core) * half, half)
    got = lax.ppermute(wanted, "col", flip)
    mine = jnp.where(pick(tk == 1, bk == 1), got, lax.dynamic_slice_in_dim(value, start, half))
    plus = col_route(lambda z, x, k: (z, x + 1, k))
    minus = col_route(lambda z, x, k: (z, x - 1, k))
    from_left = lax.ppermute(mine, "col", plus)
    from_right = lax.ppermute(mine, "col", minus)
    mine = jnp.where(pick(tx == 1, bx == 1), from_left, jnp.where(pick(tx == 3, bx == 3), from_right, mine))
    first = lax.ppermute(mine[:quarter], "col", plus)
    second = lax.ppermute(mine[quarter:], "col", minus)
    mine = jnp.where(pick(tx == 2, bx == 2), jnp.concatenate([first, second], axis=0), mine)
    got = lax.ppermute(mine, "col", col_route(lambda z, x, k: (z + 1, x, k)))
    mine = jnp.where(pick(tz == 1, bz == 1), got, mine)
    other = lax.ppermute(mine, "col", flip)
    return jnp.where(core == 0, jnp.concatenate([mine, other], axis=0), jnp.concatenate([other, mine], axis=0))


def pick(stack, index):
    mask = lax.broadcasted_iota(jnp.int32, (stack.shape[0],) + (1,) * (stack.ndim - 1), 0) == index
    return jnp.sum(jnp.where(mask, stack, jnp.zeros_like(stack)), axis=0)


def broadcast_block(block, source):
    count = lax.axis_size("col")
    piece = block.shape[0] // count
    parts = block.reshape(count, piece, block.shape[1])
    got = lax.all_to_all(parts, "col", 0, 0, tiled=False)
    early = pick(got, lax.rem(source + count - 1, count))
    late = pick(got, source)
    pair = jnp.stack([early, late])[:, ::-1]
    spread_out = jnp.broadcast_to(pair[None], (count,) + pair.shape)
    return lax.all_to_all(spread_out, "col", 0, 0, tiled=False)


def power_int(frac, exps):
    square = frac * frac
    return jnp.where(
        exps == 0,
        jnp.ones_like(frac),
        jnp.where(exps == 1, frac, jnp.where(exps == 2, square, square * frac)),
    )


def cone_matrix(lengths, exps, lags):
    rows = lengths.shape[0]
    row_pos = lax.broadcasted_iota(jnp.int32, (rows, rows + lags - 1), 0)
    col_pos = lax.broadcasted_iota(jnp.int32, (rows, rows + lags - 1), 1)
    lag = row_pos + (lags - 1) - col_pos
    span = lengths[:, None]
    valid = (lag >= 0) & (lag < span)
    inverse = 1.0 / span.astype(jnp.float32)
    frac = (span.astype(jnp.float32) - lag.astype(jnp.float32)) * inverse
    cone = jnp.where(valid, power_int(frac, exps[:, None]), jnp.zeros_like(frac))
    return cone * (1.0 / jnp.sum(cone, axis=1, keepdims=True))


def reversed_cone(lengths, exps, lags, depth):
    rows = lengths.shape[0]
    row_pos = lax.broadcasted_iota(jnp.int32, (rows, depth), 0)
    col_pos = lax.broadcasted_iota(jnp.int32, (rows, depth), 1)
    lag = row_pos + col_pos - (depth - lags) + 1
    span = lengths[:, None]
    valid = (lag >= 0) & (lag < span)
    inverse = 1.0 / span.astype(jnp.float32)
    frac = (span.astype(jnp.float32) - lag.astype(jnp.float32)) * inverse
    cone = jnp.where(valid, power_int(frac, exps[:, None]), jnp.zeros_like(frac))
    return cone * (1.0 / jnp.sum(cone, axis=1, keepdims=True))


def lag_kernel(lags, r_ref, q_ref, cp_ref, csum_ref, w_ref, o_ref):
    count = r_ref.shape[0]
    tail_count = lags // r_ref.shape[2]
    rows = jnp.concatenate(
        [r_ref[count - 1 - s, 1] for s in range(count)] + [r_ref[count - 1 - s, 0] for s in range(tail_count)],
        axis=0,
    )
    wide = rows.astype(jnp.float32)
    square = wide * wide
    row_norm = jnp.sum(square, axis=1, keepdims=True)
    inner = lax.dot_general(
        rows, q_ref[...], (((1,), (1,)), ((), ())), preferred_element_type=jnp.float32
    )
    depth = inner.shape[0]
    near = row_norm + cp_ref[...] - 2.0 * inner
    width = 2 * o_ref.shape[2]
    dist = jnp.concatenate([near, jnp.zeros((depth, width - near.shape[1]), jnp.float32)], axis=1)
    skew = pltpu.roll(dist, width - lags, 1, stride=1, stride_axis=0)
    skew_hi = skew.astype(jnp.bfloat16)
    skew_lo = (skew - skew_hi.astype(jnp.float32)).astype(jnp.bfloat16)
    weights = w_ref[...]
    w_hi = weights.astype(jnp.bfloat16)
    w_lo = (weights - w_hi.astype(jnp.float32)).astype(jnp.bfloat16)
    ones = jnp.ones((8, square.shape[1]), jnp.float32)
    norm_rows = lax.dot_general(
        ones, square, (((1,), (1,)), ((), ())), precision=lax.Precision.HIGHEST,
        preferred_element_type=jnp.float32,
    )
    row_sum = lax.dot_general(
        norm_rows, w_ref[...], (((1,), (1,)), ((), ())), precision=lax.Precision.HIGHEST,
        preferred_element_type=jnp.float32,
    )
    count, share, block = o_ref.shape[0], 64, o_ref.shape[2]
    share = block // count
    chunk = 128
    band = chunk + lags
    span = block + chunk
    for m in range(block // chunk):
        low = depth - band - chunk * m
        rows_at = slice(chunk * m, chunk * (m + 1))
        cols_at = slice(low, low + band)
        out_at = slice(low, low + span)
        part = (
            jnp.dot(w_hi[rows_at, cols_at], skew_hi[cols_at, out_at], preferred_element_type=jnp.float32)
            + jnp.dot(w_hi[rows_at, cols_at], skew_lo[cols_at, out_at], preferred_element_type=jnp.float32)
            + jnp.dot(w_lo[rows_at, cols_at], skew_hi[cols_at, out_at], preferred_element_type=jnp.float32)
        )
        lined = pltpu.roll(part, span - (chunk - 1), 1, stride=1, stride_axis=0)
        for h in range(chunk // share):
            o_ref[(chunk * m) // share + h, 0:share, :] = lined[share * h : share * (h + 1), :block]
    extra = o_ref.shape[1] - share
    tail_rows = jnp.concatenate(
        [csum_ref[...], row_sum[0:1, :], jnp.zeros((extra - 2, block), jnp.float32)], axis=0
    )
    for k in range(count):
        o_ref[k, share:, :] = tail_rows


def lag_total(row_rev, col_pad, col_norm, col_sum, weights, count, lags):
    depth = weights.shape[1]
    width = col_pad.shape[0]
    block = weights.shape[0]
    share = block // count
    flops = 2 * depth * width * col_pad.shape[1] + 6 * 2 * block * (128 + lags) * (block + 128)
    return pl.pallas_call(
        functools.partial(lag_kernel, lags),
        out_shape=jax.ShapeDtypeStruct((count, share + 8, block), jnp.float32),
        in_specs=[pl.BlockSpec(memory_space=pltpu.VMEM)] * 5,
        out_specs=pl.BlockSpec(memory_space=pltpu.VMEM),
        cost_estimate=pl.CostEstimate(
            flops=flops, transcendentals=0, bytes_accessed=4 * (block * block + block * depth) + 2 * (depth + width) * 256
        ),
    )(row_rev, col_pad, col_norm, col_sum, weights)


def shards(snapshots, offsets, window_len, cone_exp):
    block = snapshots.shape[0]
    lags = LAGS
    tail = snapshots[block - lags :]
    history = shifted(tail, "col", 1)
    col_ext = jnp.concatenate([history, snapshots], axis=0)
    chosen = pick(offsets, lax.axis_index("row"))
    pieces = broadcast_block(snapshots, chosen)
    me = lax.axis_index("col")
    extent = block + lags
    tables = jnp.stack([window_len, cone_exp]).reshape(2, -1, block).transpose(1, 0, 2)
    row_lengths, row_exps = pick(tables, chosen)
    col_lengths, col_exps = pick(tables, me)
    row_weights = reversed_cone(row_lengths, row_exps, lags, extent)
    col_weights = cone_matrix(col_lengths, col_exps, lags + 1)
    col_wide = col_ext.astype(jnp.float32)
    col_part = jnp.sum(col_wide * col_wide, axis=1)
    col_sum = jnp.sum(col_weights * col_part[None, :], axis=1)
    n_chan = lax.axis_size("chan")
    share = block // n_chan
    payload = lag_total(pieces, col_ext, col_part[None, :], col_sum[None, :], row_weights, n_chan, lags)
    mine = jnp.sum(lax.all_to_all(payload, "chan", 0, 0, tiled=False), axis=0)
    row_sum = lax.dynamic_slice_in_dim(mine[share + 1], lax.axis_index("chan") * share, share)
    row_scale = jnp.sqrt(row_sum / C + epsilon)
    col_scale = jnp.sqrt(mine[share] / C + epsilon)
    return jnp.exp(-mine[:share] / (2.0 * C * row_scale[:, None] * col_scale[None, :]))


def solution(mesh):
    in_specs = (P("col", "chan"), P(), P(), P())
    out_specs = P(("row", "chan"), "col")
    return jax.shard_map(shards, mesh=mesh, in_specs=in_specs, out_specs=out_specs, check_vma=False)
```

```python
import functools

import jax
import jax.numpy as jnp
from jax import lax
from jax.experimental import pallas as pl
from jax.experimental.pallas import tpu as pltpu
from jax.sharding import PartitionSpec as P

C = 2048
LAGS = 256


epsilon = 1e-05


def shifted(block, axis, distance):
    devices = range(lax.axis_size(axis))
    route = [((i - distance) % len(devices), i) for i in devices]
    return lax.ppermute(block, axis, route)


def spread(value, axis, source):
    kept = jnp.where(lax.axis_index(axis) == source, value, 0).astype(value.dtype)
    return lax.psum(kept, axis)


COL_PARTS = (2, 4, 2)


def col_route(step):
    outer, mid, inner = COL_PARTS
    route = []
    for c in range(outer * mid * inner):
        z, x, k = c // (mid * inner), (c // inner) % mid, c % inner
        z, x, k = step(z, x, k)
        route.append((c, (z % outer * mid + x % mid) * inner + k % inner))
    return route


def broadcast_band(tail, block, source):
    outer, mid, inner = COL_PARTS
    count = outer * mid * inner
    rows_total = tail.shape[0] + block.shape[0]
    if lax.axis_size("col") != count or mid != 4 or outer != 2 or inner != 2 or rows_total % 4 != 0:
        joined = jnp.concatenate([shifted(tail, "col", 1), block], axis=0)
        return spread(joined, "col", source)
    me = lax.axis_index("col")
    value = jnp.concatenate([tail, block], axis=0)
    split = tail.shape[0]
    half = rows_total // 2
    quarter = half // 2

    def deltas(origin):
        dz = (me // (mid * inner) - origin // (mid * inner)) % outer
        dx = ((me // inner) % mid - (origin // inner) % mid) % mid
        dk = (me % inner - origin % inner) % inner
        return dz, dx, dk

    tz, tx, tk = deltas((source + count - 1) % count)
    bz, bx, bk = deltas(source)
    core = me % inner
    start = core * half
    rows = start + lax.broadcasted_iota(jnp.int32, (half, 1), 0)

    def pick(tail_test, block_test):
        return jnp.where(rows < split, tail_test, block_test)

    flip = col_route(lambda z, x, k: (z, x, k + 1))
    wanted = lax.dynamic_slice_in_dim(value, (1 - core) * half, half)
    got = lax.ppermute(wanted, "col", flip)
    mine = jnp.where(pick(tk == 1, bk == 1), got, lax.dynamic_slice_in_dim(value, start, half))
    plus = col_route(lambda z, x, k: (z, x + 1, k))
    minus = col_route(lambda z, x, k: (z, x - 1, k))
    from_left = lax.ppermute(mine, "col", plus)
    from_right = lax.ppermute(mine, "col", minus)
    mine = jnp.where(pick(tx == 1, bx == 1), from_left, jnp.where(pick(tx == 3, bx == 3), from_right, mine))
    first = lax.ppermute(mine[:quarter], "col", plus)
    second = lax.ppermute(mine[quarter:], "col", minus)
    mine = jnp.where(pick(tx == 2, bx == 2), jnp.concatenate([first, second], axis=0), mine)
    got = lax.ppermute(mine, "col", col_route(lambda z, x, k: (z + 1, x, k)))
    mine = jnp.where(pick(tz == 1, bz == 1), got, mine)
    other = lax.ppermute(mine, "col", flip)
    return jnp.where(core == 0, jnp.concatenate([mine, other], axis=0), jnp.concatenate([other, mine], axis=0))


def pick(stack, index):
    mask = lax.broadcasted_iota(jnp.int32, (stack.shape[0],) + (1,) * (stack.ndim - 1), 0) == index
    return jnp.sum(jnp.where(mask, stack, jnp.zeros_like(stack)), axis=0)


def broadcast_block(block, source, held):
    count = lax.axis_size("col")
    piece = block.shape[0] // count
    parts = block.reshape(count, piece, block.shape[1])
    got = lax.all_to_all(parts, "col", 0, 0, tiled=False)
    got, held = lax.optimization_barrier((got, held))
    early = pick(got, lax.rem(source + count - 1, count))
    late = pick(got, source)
    pair = jnp.stack([early, late])[:, ::-1]
    spread_out = jnp.broadcast_to(pair[None], (count,) + pair.shape)
    return lax.all_to_all(spread_out, "col", 0, 0, tiled=False), held


def power_int(frac, exps):
    square = frac * frac
    return jnp.where(
        exps == 0,
        jnp.ones_like(frac),
        jnp.where(exps == 1, frac, jnp.where(exps == 2, square, square * frac)),
    )


def cone_matrix(lengths, exps, lags):
    rows = lengths.shape[0]
    row_pos = lax.broadcasted_iota(jnp.int32, (rows, rows + lags - 1), 0)
    col_pos = lax.broadcasted_iota(jnp.int32, (rows, rows + lags - 1), 1)
    lag = row_pos + (lags - 1) - col_pos
    span = lengths[:, None]
    valid = (lag >= 0) & (lag < span)
    frac = (span.astype(jnp.float32) - lag.astype(jnp.float32)) / span.astype(jnp.float32)
    cone = jnp.where(valid, power_int(frac, exps[:, None]), jnp.zeros_like(frac))
    return cone / jnp.sum(cone, axis=1, keepdims=True)


def reversed_cone(lengths, exps, lags, depth):
    rows = lengths.shape[0]
    row_pos = lax.broadcasted_iota(jnp.int32, (rows, depth), 0)
    col_pos = lax.broadcasted_iota(jnp.int32, (rows, depth), 1)
    lag = row_pos + col_pos - (depth - lags) + 1
    span = lengths[:, None]
    valid = (lag >= 0) & (lag < span)
    frac = (span.astype(jnp.float32) - lag.astype(jnp.float32)) / span.astype(jnp.float32)
    cone = jnp.where(valid, power_int(frac, exps[:, None]), jnp.zeros_like(frac))
    return cone / jnp.sum(cone, axis=1, keepdims=True)


def lag_kernel(lags, r_ref, q_ref, cp_ref, csum_ref, w_ref, o_ref):
    count = r_ref.shape[0]
    tail_count = lags // r_ref.shape[2]
    rows = jnp.concatenate(
        [r_ref[count - 1 - s, 1] for s in range(count)] + [r_ref[count - 1 - s, 0] for s in range(tail_count)],
        axis=0,
    )
    wide = rows.astype(jnp.float32)
    square = wide * wide
    row_norm = jnp.sum(square, axis=1, keepdims=True)
    inner = lax.dot_general(
        rows, q_ref[...], (((1,), (1,)), ((), ())), preferred_element_type=jnp.float32
    )
    depth = inner.shape[0]
    near = row_norm + cp_ref[...] - 2.0 * inner
    width = 2 * o_ref.shape[2]
    dist = jnp.concatenate([near, jnp.zeros((depth, width - near.shape[1]), jnp.float32)], axis=1)
    skew = pltpu.roll(dist, width - lags, 1, stride=1, stride_axis=0)
    skew_hi = skew.astype(jnp.bfloat16)
    skew_lo = (skew - skew_hi.astype(jnp.float32)).astype(jnp.bfloat16)
    weights = w_ref[...]
    w_hi = weights.astype(jnp.bfloat16)
    w_lo = (weights - w_hi.astype(jnp.float32)).astype(jnp.bfloat16)
    ones = jnp.ones((8, square.shape[1]), jnp.float32)
    norm_rows = lax.dot_general(
        ones, square, (((1,), (1,)), ((), ())), precision=lax.Precision.HIGHEST,
        preferred_element_type=jnp.float32,
    )
    row_sum = lax.dot_general(
        norm_rows, w_ref[...], (((1,), (1,)), ((), ())), precision=lax.Precision.HIGHEST,
        preferred_element_type=jnp.float32,
    )
    count, share, block = o_ref.shape[0], 64, o_ref.shape[2]
    share = block // count
    chunk = 128
    band = chunk + lags
    span = block + chunk
    for m in range(block // chunk):
        low = depth - band - chunk * m
        rows_at = slice(chunk * m, chunk * (m + 1))
        cols_at = slice(low, low + band)
        out_at = slice(low, low + span)
        part = (
            jnp.dot(w_hi[rows_at, cols_at], skew_hi[cols_at, out_at], preferred_element_type=jnp.float32)
            + jnp.dot(w_hi[rows_at, cols_at], skew_lo[cols_at, out_at], preferred_element_type=jnp.float32)
            + jnp.dot(w_lo[rows_at, cols_at], skew_hi[cols_at, out_at], preferred_element_type=jnp.float32)
        )
        lined = pltpu.roll(part, span - (chunk - 1), 1, stride=1, stride_axis=0)
        for h in range(chunk // share):
            o_ref[(chunk * m) // share + h, 0:share, :] = lined[share * h : share * (h + 1), :block]
    extra = o_ref.shape[1] - share
    tail_rows = jnp.concatenate(
        [csum_ref[...], row_sum[0:1, :], jnp.zeros((extra - 2, block), jnp.float32)], axis=0
    )
    for k in range(count):
        o_ref[k, share:, :] = tail_rows


def lag_total(row_rev, col_pad, col_norm, col_sum, weights, count, lags):
    depth = weights.shape[1]
    width = col_pad.shape[0]
    block = weights.shape[0]
    share = block // count
    flops = 2 * depth * width * col_pad.shape[1] + 6 * 2 * block * (128 + lags) * (block + 128)
    return pl.pallas_call(
        functools.partial(lag_kernel, lags),
        out_shape=jax.ShapeDtypeStruct((count, share + 8, block), jnp.float32),
        in_specs=[pl.BlockSpec(memory_space=pltpu.VMEM)] * 5,
        out_specs=pl.BlockSpec(memory_space=pltpu.VMEM),
        cost_estimate=pl.CostEstimate(
            flops=flops, transcendentals=0, bytes_accessed=4 * (block * block + block * depth) + 2 * (depth + width) * 256
        ),
    )(row_rev, col_pad, col_norm, col_sum, weights)


def shards(snapshots, offsets, window_len, cone_exp):
    block = snapshots.shape[0]
    lags = LAGS
    tail = snapshots[block - lags :]
    history = shifted(tail, "col", 1)
    col_ext = jnp.concatenate([history, snapshots], axis=0)
    chosen = pick(offsets, lax.axis_index("row"))
    me = lax.axis_index("col")
    extent = block + lags
    lengths = window_len.reshape(-1, block)
    exps = cone_exp.reshape(-1, block)
    pieces, (col_lengths, col_exps) = broadcast_block(snapshots, chosen, (pick(lengths, me), pick(exps, me)))
    row_weights = reversed_cone(pick(lengths, chosen), pick(exps, chosen), lags, extent)
    col_weights = cone_matrix(col_lengths, col_exps, lags + 1)
    col_wide = col_ext.astype(jnp.float32)
    col_part = jnp.sum(col_wide * col_wide, axis=1)
    col_sum = jnp.sum(col_weights * col_part[None, :], axis=1)
    n_chan = lax.axis_size("chan")
    share = block // n_chan
    payload = lag_total(pieces, col_ext, col_part[None, :], col_sum[None, :], row_weights, n_chan, lags)
    mine = jnp.sum(lax.all_to_all(payload, "chan", 0, 0, tiled=False), axis=0)
    row_sum = lax.dynamic_slice_in_dim(mine[share + 1], lax.axis_index("chan") * share, share)
    row_scale = jnp.sqrt(row_sum / C + epsilon)
    col_scale = jnp.sqrt(mine[share] / C + epsilon)
    return jnp.exp(-mine[:share] / (2.0 * C * row_scale[:, None] * col_scale[None, :]))


def solution(mesh):
    in_specs = (P("col", "chan"), P(), P(), P())
    out_specs = P(("row", "chan"), "col")
    return jax.shard_map(shards, mesh=mesh, in_specs=in_specs, out_specs=out_specs, check_vma=False)
```

```python
import functools

import jax
import jax.numpy as jnp
from jax import lax
from jax.experimental import pallas as pl
from jax.experimental.pallas import tpu as pltpu
from jax.sharding import PartitionSpec as P

C = 2048
LAGS = 256


epsilon = 1e-05


def shifted(block, axis, distance):
    devices = range(lax.axis_size(axis))
    route = [((i - distance) % len(devices), i) for i in devices]
    return lax.ppermute(block, axis, route)


def spread(value, axis, source):
    kept = jnp.where(lax.axis_index(axis) == source, value, 0).astype(value.dtype)
    return lax.psum(kept, axis)


COL_PARTS = (2, 4, 2)


def col_route(step):
    outer, mid, inner = COL_PARTS
    route = []
    for c in range(outer * mid * inner):
        z, x, k = c // (mid * inner), (c // inner) % mid, c % inner
        z, x, k = step(z, x, k)
        route.append((c, (z % outer * mid + x % mid) * inner + k % inner))
    return route


def broadcast_band(tail, block, source):
    outer, mid, inner = COL_PARTS
    count = outer * mid * inner
    rows_total = tail.shape[0] + block.shape[0]
    if lax.axis_size("col") != count or mid != 4 or outer != 2 or inner != 2 or rows_total % 4 != 0:
        joined = jnp.concatenate([shifted(tail, "col", 1), block], axis=0)
        return spread(joined, "col", source)
    me = lax.axis_index("col")
    value = jnp.concatenate([tail, block], axis=0)
    split = tail.shape[0]
    half = rows_total // 2
    quarter = half // 2

    def deltas(origin):
        dz = (me // (mid * inner) - origin // (mid * inner)) % outer
        dx = ((me // inner) % mid - (origin // inner) % mid) % mid
        dk = (me % inner - origin % inner) % inner
        return dz, dx, dk

    tz, tx, tk = deltas((source + count - 1) % count)
    bz, bx, bk = deltas(source)
    core = me % inner
    start = core * half
    rows = start + lax.broadcasted_iota(jnp.int32, (half, 1), 0)

    def pick(tail_test, block_test):
        return jnp.where(rows < split, tail_test, block_test)

    flip = col_route(lambda z, x, k: (z, x, k + 1))
    wanted = lax.dynamic_slice_in_dim(value, (1 - core) * half, half)
    got = lax.ppermute(wanted, "col", flip)
    mine = jnp.where(pick(tk == 1, bk == 1), got, lax.dynamic_slice_in_dim(value, start, half))
    plus = col_route(lambda z, x, k: (z, x + 1, k))
    minus = col_route(lambda z, x, k: (z, x - 1, k))
    from_left = lax.ppermute(mine, "col", plus)
    from_right = lax.ppermute(mine, "col", minus)
    mine = jnp.where(pick(tx == 1, bx == 1), from_left, jnp.where(pick(tx == 3, bx == 3), from_right, mine))
    first = lax.ppermute(mine[:quarter], "col", plus)
    second = lax.ppermute(mine[quarter:], "col", minus)
    mine = jnp.where(pick(tx == 2, bx == 2), jnp.concatenate([first, second], axis=0), mine)
    got = lax.ppermute(mine, "col", col_route(lambda z, x, k: (z + 1, x, k)))
    mine = jnp.where(pick(tz == 1, bz == 1), got, mine)
    other = lax.ppermute(mine, "col", flip)
    return jnp.where(core == 0, jnp.concatenate([mine, other], axis=0), jnp.concatenate([other, mine], axis=0))


def pick(stack, index):
    mask = lax.broadcasted_iota(jnp.int32, (stack.shape[0],) + (1,) * (stack.ndim - 1), 0) == index
    return jnp.sum(jnp.where(mask, stack, jnp.zeros_like(stack)), axis=0)


def broadcast_block(block, source):
    count = lax.axis_size("col")
    piece = block.shape[0] // count
    parts = block.reshape(count, piece, block.shape[1])
    got = lax.all_to_all(parts, "col", 0, 0, tiled=False)
    early = pick(got, lax.rem(source + count - 1, count))
    late = pick(got, source)
    pair = jnp.stack([early, late])[:, ::-1]
    spread_out = jnp.broadcast_to(pair[None], (count,) + pair.shape)
    return lax.all_to_all(spread_out, "col", 0, 0, tiled=False)


def power_int(frac, exps):
    square = frac * frac
    return jnp.where(
        exps == 0,
        jnp.ones_like(frac),
        jnp.where(exps == 1, frac, jnp.where(exps == 2, square, square * frac)),
    )


def cone_matrix(lengths, exps, lags):
    rows = lengths.shape[0]
    row_pos = lax.broadcasted_iota(jnp.int32, (rows, rows + lags - 1), 0)
    col_pos = lax.broadcasted_iota(jnp.int32, (rows, rows + lags - 1), 1)
    lag = row_pos + (lags - 1) - col_pos
    span = lengths[:, None]
    valid = (lag >= 0) & (lag < span)
    frac = (span.astype(jnp.float32) - lag.astype(jnp.float32)) / span.astype(jnp.float32)
    cone = jnp.where(valid, power_int(frac, exps[:, None]), jnp.zeros_like(frac))
    return cone / jnp.sum(cone, axis=1, keepdims=True)


def reversed_cone(lengths, exps, lags, depth):
    rows = lengths.shape[0]
    row_pos = lax.broadcasted_iota(jnp.int32, (rows, depth), 0)
    col_pos = lax.broadcasted_iota(jnp.int32, (rows, depth), 1)
    lag = row_pos + col_pos - (depth - lags) + 1
    span = lengths[:, None]
    valid = (lag >= 0) & (lag < span)
    frac = (span.astype(jnp.float32) - lag.astype(jnp.float32)) / span.astype(jnp.float32)
    cone = jnp.where(valid, power_int(frac, exps[:, None]), jnp.zeros_like(frac))
    return cone / jnp.sum(cone, axis=1, keepdims=True)


def lag_kernel(lags, r_ref, q_ref, cp_ref, csum_ref, w_ref, o_ref):
    count = r_ref.shape[0]
    tail_count = lags // r_ref.shape[2]
    rows = jnp.concatenate(
        [r_ref[count - 1 - s, 1] for s in range(count)] + [r_ref[count - 1 - s, 0] for s in range(tail_count)],
        axis=0,
    )
    wide = rows.astype(jnp.float32)
    square = wide * wide
    row_norm = jnp.sum(square, axis=1, keepdims=True)
    inner = lax.dot_general(
        rows, q_ref[...], (((1,), (1,)), ((), ())), preferred_element_type=jnp.float32
    )
    depth = inner.shape[0]
    near = row_norm + cp_ref[...] - 2.0 * inner
    width = 2 * o_ref.shape[2]
    dist = jnp.concatenate([near, jnp.zeros((depth, width - near.shape[1]), jnp.float32)], axis=1)
    skew = pltpu.roll(dist, width - lags, 1, stride=1, stride_axis=0)
    skew_hi = skew.astype(jnp.bfloat16)
    skew_lo = (skew - skew_hi.astype(jnp.float32)).astype(jnp.bfloat16)
    weights = w_ref[...]
    w_hi = weights.astype(jnp.bfloat16)
    w_lo = (weights - w_hi.astype(jnp.float32)).astype(jnp.bfloat16)
    ones = jnp.ones((8, square.shape[1]), jnp.float32)
    norm_rows = lax.dot_general(
        ones, square, (((1,), (1,)), ((), ())), precision=lax.Precision.HIGHEST,
        preferred_element_type=jnp.float32,
    )
    row_sum = lax.dot_general(
        norm_rows, w_ref[...], (((1,), (1,)), ((), ())), precision=lax.Precision.HIGHEST,
        preferred_element_type=jnp.float32,
    )
    count, share, block = o_ref.shape[0], 64, o_ref.shape[2]
    share = block // count
    chunk = 128
    band = chunk + lags
    span = block + chunk
    for m in range(block // chunk):
        low = depth - band - chunk * m
        rows_at = slice(chunk * m, chunk * (m + 1))
        cols_at = slice(low, low + band)
        out_at = slice(low, low + span)
        part = (
            jnp.dot(w_hi[rows_at, cols_at], skew_hi[cols_at, out_at], preferred_element_type=jnp.float32)
            + jnp.dot(w_hi[rows_at, cols_at], skew_lo[cols_at, out_at], preferred_element_type=jnp.float32)
            + jnp.dot(w_lo[rows_at, cols_at], skew_hi[cols_at, out_at], preferred_element_type=jnp.float32)
        )
        lined = pltpu.roll(part, span - (chunk - 1), 1, stride=1, stride_axis=0)
        for h in range(chunk // share):
            o_ref[(chunk * m) // share + h, 0:share, :] = lined[share * h : share * (h + 1), :block]
    extra = o_ref.shape[1] - share
    tail_rows = jnp.concatenate(
        [csum_ref[...], row_sum[0:1, :], jnp.zeros((extra - 2, block), jnp.float32)], axis=0
    )
    for k in range(count):
        o_ref[k, share:, :] = tail_rows


def lag_total(row_rev, col_pad, col_norm, col_sum, weights, count, lags):
    depth = weights.shape[1]
    width = col_pad.shape[0]
    block = weights.shape[0]
    share = block // count
    flops = 2 * depth * width * col_pad.shape[1] + 6 * 2 * block * (128 + lags) * (block + 128)
    return pl.pallas_call(
        functools.partial(lag_kernel, lags),
        out_shape=jax.ShapeDtypeStruct((count, share + 8, block), jnp.float32),
        in_specs=[pl.BlockSpec(memory_space=pltpu.VMEM)] * 5,
        out_specs=pl.BlockSpec(memory_space=pltpu.VMEM),
        cost_estimate=pl.CostEstimate(
            flops=flops, transcendentals=0, bytes_accessed=4 * (block * block + block * depth) + 2 * (depth + width) * 256
        ),
    )(row_rev, col_pad, col_norm, col_sum, weights)


def shards(snapshots, offsets, window_len, cone_exp):
    block = snapshots.shape[0]
    lags = LAGS
    history = shifted(snapshots, "col", 1)[block - lags :]
    col_ext = jnp.concatenate([history, snapshots], axis=0)
    chosen = pick(offsets, lax.axis_index("row"))
    pieces = broadcast_block(snapshots, chosen)
    me = lax.axis_index("col")
    extent = block + lags
    lengths = window_len.reshape(-1, block)
    exps = cone_exp.reshape(-1, block)
    row_weights = reversed_cone(pick(lengths, chosen), pick(exps, chosen), lags, extent)
    col_weights = cone_matrix(pick(lengths, me), pick(exps, me), lags + 1)
    col_wide = col_ext.astype(jnp.float32)
    col_part = jnp.sum(col_wide * col_wide, axis=1)
    col_sum = jnp.sum(col_weights * col_part[None, :], axis=1)
    n_chan = lax.axis_size("chan")
    share = block // n_chan
    payload = lag_total(pieces, col_ext, col_part[None, :], col_sum[None, :], row_weights, n_chan, lags)
    mine = jnp.sum(lax.all_to_all(payload, "chan", 0, 0, tiled=False), axis=0)
    row_sum = lax.dynamic_slice_in_dim(mine[share + 1], lax.axis_index("chan") * share, share)
    row_scale = jnp.sqrt(row_sum / C + epsilon)
    col_scale = jnp.sqrt(mine[share] / C + epsilon)
    return jnp.exp(-mine[:share] / (2.0 * C * row_scale[:, None] * col_scale[None, :]))


def solution(mesh):
    in_specs = (P("col", "chan"), P(), P(), P())
    out_specs = P(("row", "chan"), "col")
    return jax.shard_map(shards, mesh=mesh, in_specs=in_specs, out_specs=out_specs, check_vma=False)
```

```python
import functools

import jax
import jax.numpy as jnp
from jax import lax
from jax.experimental import pallas as pl
from jax.experimental.pallas import tpu as pltpu
from jax.sharding import PartitionSpec as P

C = 2048
LAGS = 256


epsilon = 1e-05


def shifted(block, axis, distance):
    devices = range(lax.axis_size(axis))
    route = [((i - distance) % len(devices), i) for i in devices]
    return lax.ppermute(block, axis, route)


def spread(value, axis, source):
    kept = jnp.where(lax.axis_index(axis) == source, value, 0).astype(value.dtype)
    return lax.psum(kept, axis)


COL_PARTS = (2, 4, 2)


def col_route(step):
    outer, mid, inner = COL_PARTS
    route = []
    for c in range(outer * mid * inner):
        z, x, k = c // (mid * inner), (c // inner) % mid, c % inner
        z, x, k = step(z, x, k)
        route.append((c, (z % outer * mid + x % mid) * inner + k % inner))
    return route


def broadcast_band(tail, block, source):
    outer, mid, inner = COL_PARTS
    count = outer * mid * inner
    rows_total = tail.shape[0] + block.shape[0]
    if lax.axis_size("col") != count or mid != 4 or outer != 2 or inner != 2 or rows_total % 4 != 0:
        joined = jnp.concatenate([shifted(tail, "col", 1), block], axis=0)
        return spread(joined, "col", source)
    me = lax.axis_index("col")
    value = jnp.concatenate([tail, block], axis=0)
    split = tail.shape[0]
    half = rows_total // 2
    quarter = half // 2

    def deltas(origin):
        dz = (me // (mid * inner) - origin // (mid * inner)) % outer
        dx = ((me // inner) % mid - (origin // inner) % mid) % mid
        dk = (me % inner - origin % inner) % inner
        return dz, dx, dk

    tz, tx, tk = deltas((source + count - 1) % count)
    bz, bx, bk = deltas(source)
    core = me % inner
    start = core * half
    rows = start + lax.broadcasted_iota(jnp.int32, (half, 1), 0)

    def pick(tail_test, block_test):
        return jnp.where(rows < split, tail_test, block_test)

    flip = col_route(lambda z, x, k: (z, x, k + 1))
    wanted = lax.dynamic_slice_in_dim(value, (1 - core) * half, half)
    got = lax.ppermute(wanted, "col", flip)
    mine = jnp.where(pick(tk == 1, bk == 1), got, lax.dynamic_slice_in_dim(value, start, half))
    plus = col_route(lambda z, x, k: (z, x + 1, k))
    minus = col_route(lambda z, x, k: (z, x - 1, k))
    from_left = lax.ppermute(mine, "col", plus)
    from_right = lax.ppermute(mine, "col", minus)
    mine = jnp.where(pick(tx == 1, bx == 1), from_left, jnp.where(pick(tx == 3, bx == 3), from_right, mine))
    first = lax.ppermute(mine[:quarter], "col", plus)
    second = lax.ppermute(mine[quarter:], "col", minus)
    mine = jnp.where(pick(tx == 2, bx == 2), jnp.concatenate([first, second], axis=0), mine)
    got = lax.ppermute(mine, "col", col_route(lambda z, x, k: (z + 1, x, k)))
    mine = jnp.where(pick(tz == 1, bz == 1), got, mine)
    other = lax.ppermute(mine, "col", flip)
    return jnp.where(core == 0, jnp.concatenate([mine, other], axis=0), jnp.concatenate([other, mine], axis=0))


def pick(stack, index):
    mask = lax.broadcasted_iota(jnp.int32, (stack.shape[0],) + (1,) * (stack.ndim - 1), 0) == index
    return jnp.sum(jnp.where(mask, stack, jnp.zeros_like(stack)), axis=0)


def broadcast_block(block, source):
    count = lax.axis_size("col")
    piece = block.shape[0] // count
    parts = block.reshape(count, piece, block.shape[1])
    got = lax.all_to_all(parts, "col", 0, 0, tiled=False)
    early = pick(got, lax.rem(source + count - 1, count))
    late = pick(got, source)
    pair = jnp.stack([early, late])[:, ::-1]
    spread_out = jnp.broadcast_to(pair[None], (count,) + pair.shape)
    return lax.all_to_all(spread_out, "col", 0, 0, tiled=False)


def power_int(frac, exps):
    square = frac * frac
    return jnp.where(
        exps == 0,
        jnp.ones_like(frac),
        jnp.where(exps == 1, frac, jnp.where(exps == 2, square, square * frac)),
    )


def cone_matrix(lengths, exps, lags):
    rows = lengths.shape[0]
    row_pos = lax.broadcasted_iota(jnp.int32, (rows, rows + lags - 1), 0)
    col_pos = lax.broadcasted_iota(jnp.int32, (rows, rows + lags - 1), 1)
    lag = row_pos + (lags - 1) - col_pos
    span = lengths[:, None]
    valid = (lag >= 0) & (lag < span)
    frac = (span.astype(jnp.float32) - lag.astype(jnp.float32)) / span.astype(jnp.float32)
    cone = jnp.where(valid, power_int(frac, exps[:, None]), jnp.zeros_like(frac))
    return cone / jnp.sum(cone, axis=1, keepdims=True)


def reversed_cone(lengths, exps, lags, depth):
    rows = lengths.shape[0]
    row_pos = lax.broadcasted_iota(jnp.int32, (rows, depth), 0)
    col_pos = lax.broadcasted_iota(jnp.int32, (rows, depth), 1)
    lag = row_pos + col_pos - (depth - lags) + 1
    span = lengths[:, None]
    valid = (lag >= 0) & (lag < span)
    frac = (span.astype(jnp.float32) - lag.astype(jnp.float32)) / span.astype(jnp.float32)
    cone = jnp.where(valid, power_int(frac, exps[:, None]), jnp.zeros_like(frac))
    return cone / jnp.sum(cone, axis=1, keepdims=True)


def lag_kernel(lags, r_ref, q_ref, cp_ref, csum_ref, w_ref, o_ref):
    count = r_ref.shape[0]
    tail_count = lags // r_ref.shape[2]
    rows = jnp.concatenate(
        [r_ref[count - 1 - s, 1] for s in range(count)] + [r_ref[count - 1 - s, 0] for s in range(tail_count)],
        axis=0,
    )
    wide = rows.astype(jnp.float32)
    square = wide * wide
    row_norm = jnp.sum(square, axis=1, keepdims=True)
    inner = lax.dot_general(
        rows, q_ref[...], (((1,), (1,)), ((), ())), preferred_element_type=jnp.float32
    )
    depth = inner.shape[0]
    near = row_norm + cp_ref[...] - 2.0 * inner
    width = 2 * o_ref.shape[2]
    dist = jnp.concatenate([near, jnp.zeros((depth, width - near.shape[1]), jnp.float32)], axis=1)
    skew = pltpu.roll(dist, width - lags, 1, stride=1, stride_axis=0)
    skew_hi = skew.astype(jnp.bfloat16)
    skew_lo = (skew - skew_hi.astype(jnp.float32)).astype(jnp.bfloat16)
    weights = w_ref[...]
    w_hi = weights.astype(jnp.bfloat16)
    w_lo = (weights - w_hi.astype(jnp.float32)).astype(jnp.bfloat16)
    ones = jnp.ones((8, square.shape[1]), jnp.bfloat16)
    square_hi = square.astype(jnp.bfloat16)
    square_lo = (square - square_hi.astype(jnp.float32)).astype(jnp.bfloat16)
    contract = (((1,), (1,)), ((), ()))
    norm_rows = lax.dot_general(ones, square_hi, contract, preferred_element_type=jnp.float32) + lax.dot_general(
        ones, square_lo, contract, preferred_element_type=jnp.float32
    )
    norm_hi = norm_rows.astype(jnp.bfloat16)
    norm_lo = (norm_rows - norm_hi.astype(jnp.float32)).astype(jnp.bfloat16)
    row_sum = (
        lax.dot_general(norm_hi, w_hi, contract, preferred_element_type=jnp.float32)
        + lax.dot_general(norm_hi, w_lo, contract, preferred_element_type=jnp.float32)
        + lax.dot_general(norm_lo, w_hi, contract, preferred_element_type=jnp.float32)
    )
    count, share, block = o_ref.shape[0], 64, o_ref.shape[2]
    share = block // count
    chunk = 128
    band = chunk + lags
    span = block + chunk
    for m in range(block // chunk):
        low = depth - band - chunk * m
        rows_at = slice(chunk * m, chunk * (m + 1))
        cols_at = slice(low, low + band)
        out_at = slice(low, low + span)
        part = (
            jnp.dot(w_hi[rows_at, cols_at], skew_hi[cols_at, out_at], preferred_element_type=jnp.float32)
            + jnp.dot(w_hi[rows_at, cols_at], skew_lo[cols_at, out_at], preferred_element_type=jnp.float32)
            + jnp.dot(w_lo[rows_at, cols_at], skew_hi[cols_at, out_at], preferred_element_type=jnp.float32)
        )
        lined = pltpu.roll(part, span - (chunk - 1), 1, stride=1, stride_axis=0)
        for h in range(chunk // share):
            o_ref[(chunk * m) // share + h, 0:share, :] = lined[share * h : share * (h + 1), :block]
    extra = o_ref.shape[1] - share
    tail_rows = jnp.concatenate(
        [csum_ref[...], row_sum[0:1, :], jnp.zeros((extra - 2, block), jnp.float32)], axis=0
    )
    for k in range(count):
        o_ref[k, share:, :] = tail_rows


def lag_total(row_rev, col_pad, col_norm, col_sum, weights, count, lags):
    depth = weights.shape[1]
    width = col_pad.shape[0]
    block = weights.shape[0]
    share = block // count
    flops = 2 * depth * width * col_pad.shape[1] + 6 * 2 * block * (128 + lags) * (block + 128)
    return pl.pallas_call(
        functools.partial(lag_kernel, lags),
        out_shape=jax.ShapeDtypeStruct((count, share + 8, block), jnp.float32),
        in_specs=[pl.BlockSpec(memory_space=pltpu.VMEM)] * 5,
        out_specs=pl.BlockSpec(memory_space=pltpu.VMEM),
        cost_estimate=pl.CostEstimate(
            flops=flops, transcendentals=0, bytes_accessed=4 * (block * block + block * depth) + 2 * (depth + width) * 256
        ),
    )(row_rev, col_pad, col_norm, col_sum, weights)


def shards(snapshots, offsets, window_len, cone_exp):
    block = snapshots.shape[0]
    lags = LAGS
    history = shifted(snapshots, "col", 1)[block - lags :]
    col_ext = jnp.concatenate([history, snapshots], axis=0)
    chosen = pick(offsets, lax.axis_index("row"))
    pieces = broadcast_block(snapshots, chosen)
    me = lax.axis_index("col")
    extent = block + lags
    lengths = window_len.reshape(-1, block)
    exps = cone_exp.reshape(-1, block)
    row_weights = reversed_cone(pick(lengths, chosen), pick(exps, chosen), lags, extent)
    col_weights = cone_matrix(pick(lengths, me), pick(exps, me), lags + 1)
    col_wide = col_ext.astype(jnp.float32)
    col_part = jnp.sum(col_wide * col_wide, axis=1)
    col_sum = jnp.sum(col_weights * col_part[None, :], axis=1)
    n_chan = lax.axis_size("chan")
    share = block // n_chan
    payload = lag_total(pieces, col_ext, col_part[None, :], col_sum[None, :], row_weights, n_chan, lags)
    mine = jnp.sum(lax.all_to_all(payload, "chan", 0, 0, tiled=False), axis=0)
    row_sum = lax.dynamic_slice_in_dim(mine[share + 1], lax.axis_index("chan") * share, share)
    row_scale = jnp.sqrt(row_sum / C + epsilon)
    col_scale = jnp.sqrt(mine[share] / C + epsilon)
    return jnp.exp(-mine[:share] / (2.0 * C * row_scale[:, None] * col_scale[None, :]))


def solution(mesh):
    in_specs = (P("col", "chan"), P(), P(), P())
    out_specs = P(("row", "chan"), "col")
    return jax.shard_map(shards, mesh=mesh, in_specs=in_specs, out_specs=out_specs, check_vma=False)
```

```python
import functools

import jax
import jax.numpy as jnp
from jax import lax
from jax.experimental import pallas as pl
from jax.experimental.pallas import tpu as pltpu
from jax.sharding import PartitionSpec as P

C = 2048
LAGS = 256


epsilon = 1e-05


def shifted(block, axis, distance):
    devices = range(lax.axis_size(axis))
    route = [((i - distance) % len(devices), i) for i in devices]
    return lax.ppermute(block, axis, route)


def spread(value, axis, source):
    kept = jnp.where(lax.axis_index(axis) == source, value, 0).astype(value.dtype)
    return lax.psum(kept, axis)


COL_PARTS = (2, 4, 2)


def col_route(step):
    outer, mid, inner = COL_PARTS
    route = []
    for c in range(outer * mid * inner):
        z, x, k = c // (mid * inner), (c // inner) % mid, c % inner
        z, x, k = step(z, x, k)
        route.append((c, (z % outer * mid + x % mid) * inner + k % inner))
    return route


def broadcast_band(tail, block, source):
    outer, mid, inner = COL_PARTS
    count = outer * mid * inner
    rows_total = tail.shape[0] + block.shape[0]
    if lax.axis_size("col") != count or mid != 4 or outer != 2 or inner != 2 or rows_total % 4 != 0:
        joined = jnp.concatenate([shifted(tail, "col", 1), block], axis=0)
        return spread(joined, "col", source)
    me = lax.axis_index("col")
    value = jnp.concatenate([tail, block], axis=0)
    split = tail.shape[0]
    half = rows_total // 2
    quarter = half // 2

    def deltas(origin):
        dz = (me // (mid * inner) - origin // (mid * inner)) % outer
        dx = ((me // inner) % mid - (origin // inner) % mid) % mid
        dk = (me % inner - origin % inner) % inner
        return dz, dx, dk

    tz, tx, tk = deltas((source + count - 1) % count)
    bz, bx, bk = deltas(source)
    core = me % inner
    start = core * half
    rows = start + lax.broadcasted_iota(jnp.int32, (half, 1), 0)

    def pick(tail_test, block_test):
        return jnp.where(rows < split, tail_test, block_test)

    flip = col_route(lambda z, x, k: (z, x, k + 1))
    wanted = lax.dynamic_slice_in_dim(value, (1 - core) * half, half)
    got = lax.ppermute(wanted, "col", flip)
    mine = jnp.where(pick(tk == 1, bk == 1), got, lax.dynamic_slice_in_dim(value, start, half))
    plus = col_route(lambda z, x, k: (z, x + 1, k))
    minus = col_route(lambda z, x, k: (z, x - 1, k))
    from_left = lax.ppermute(mine, "col", plus)
    from_right = lax.ppermute(mine, "col", minus)
    mine = jnp.where(pick(tx == 1, bx == 1), from_left, jnp.where(pick(tx == 3, bx == 3), from_right, mine))
    first = lax.ppermute(mine[:quarter], "col", plus)
    second = lax.ppermute(mine[quarter:], "col", minus)
    mine = jnp.where(pick(tx == 2, bx == 2), jnp.concatenate([first, second], axis=0), mine)
    got = lax.ppermute(mine, "col", col_route(lambda z, x, k: (z + 1, x, k)))
    mine = jnp.where(pick(tz == 1, bz == 1), got, mine)
    other = lax.ppermute(mine, "col", flip)
    return jnp.where(core == 0, jnp.concatenate([mine, other], axis=0), jnp.concatenate([other, mine], axis=0))


def pick(stack, index):
    mask = lax.broadcasted_iota(jnp.int32, (stack.shape[0],) + (1,) * (stack.ndim - 1), 0) == index
    return jnp.sum(jnp.where(mask, stack, jnp.zeros_like(stack)), axis=0)


def broadcast_block(block, source):
    count = lax.axis_size("col")
    piece = block.shape[0] // count
    parts = block.reshape(count, piece, block.shape[1])
    got = lax.all_to_all(parts, "col", 0, 0, tiled=False)
    early = pick(got, lax.rem(source + count - 1, count))
    late = pick(got, source)
    pair = jnp.stack([early, late])[:, ::-1]
    spread_out = jnp.broadcast_to(pair[None], (count,) + pair.shape)
    return lax.all_to_all(spread_out, "col", 0, 0, tiled=False)


def power_int(frac, exps):
    square = frac * frac
    return jnp.where(
        exps == 0,
        jnp.ones_like(frac),
        jnp.where(exps == 1, frac, jnp.where(exps == 2, square, square * frac)),
    )


def cone_matrix(lengths, exps, lags):
    rows = lengths.shape[0]
    row_pos = lax.broadcasted_iota(jnp.int32, (rows, rows + lags - 1), 0)
    col_pos = lax.broadcasted_iota(jnp.int32, (rows, rows + lags - 1), 1)
    lag = row_pos + (lags - 1) - col_pos
    span = lengths[:, None]
    valid = (lag >= 0) & (lag < span)
    frac = (span.astype(jnp.float32) - lag.astype(jnp.float32)) / span.astype(jnp.float32)
    cone = jnp.where(valid, power_int(frac, exps[:, None]), jnp.zeros_like(frac))
    return cone / jnp.sum(cone, axis=1, keepdims=True)


def reversed_cone(lengths, exps, lags, depth):
    rows = lengths.shape[0]
    row_pos = lax.broadcasted_iota(jnp.int32, (rows, depth), 0)
    col_pos = lax.broadcasted_iota(jnp.int32, (rows, depth), 1)
    lag = row_pos + col_pos - (depth - lags) + 1
    span = lengths[:, None]
    valid = (lag >= 0) & (lag < span)
    frac = (span.astype(jnp.float32) - lag.astype(jnp.float32)) / span.astype(jnp.float32)
    cone = jnp.where(valid, power_int(frac, exps[:, None]), jnp.zeros_like(frac))
    return cone / jnp.sum(cone, axis=1, keepdims=True)


def lag_kernel(lags, r_ref, q_ref, cp_ref, csum_ref, w_ref, o_ref):
    count = r_ref.shape[0]
    tail_count = lags // r_ref.shape[2]
    rows = jnp.concatenate(
        [r_ref[count - 1 - s, 1] for s in range(count)] + [r_ref[count - 1 - s, 0] for s in range(tail_count)],
        axis=0,
    )
    wide = rows.astype(jnp.float32)
    square = wide * wide
    row_norm = jnp.sum(square, axis=1, keepdims=True)
    inner = lax.dot_general(
        rows, q_ref[...], (((1,), (1,)), ((), ())), preferred_element_type=jnp.float32
    )
    depth = inner.shape[0]
    near = row_norm + cp_ref[...] - 2.0 * inner
    width = 2 * o_ref.shape[2]
    dist = jnp.concatenate([near, jnp.zeros((depth, width - near.shape[1]), jnp.float32)], axis=1)
    skew = pltpu.roll(dist, width - lags, 1, stride=1, stride_axis=0)
    skew_hi = skew.astype(jnp.bfloat16)
    skew_lo = (skew - skew_hi.astype(jnp.float32)).astype(jnp.bfloat16)
    weights = w_ref[...]
    w_hi = weights.astype(jnp.bfloat16)
    w_lo = (weights - w_hi.astype(jnp.float32)).astype(jnp.bfloat16)
    ones = jnp.ones((8, square.shape[1]), jnp.bfloat16)
    square_hi = square.astype(jnp.bfloat16)
    square_lo = (square - square_hi.astype(jnp.float32)).astype(jnp.bfloat16)
    contract = (((1,), (1,)), ((), ()))
    norm_rows = lax.dot_general(ones, square_hi, contract, preferred_element_type=jnp.float32) + lax.dot_general(
        ones, square_lo, contract, preferred_element_type=jnp.float32
    )
    norm_hi = norm_rows.astype(jnp.bfloat16)
    norm_lo = (norm_rows - norm_hi.astype(jnp.float32)).astype(jnp.bfloat16)
    row_sum = (
        lax.dot_general(norm_hi, w_hi, contract, preferred_element_type=jnp.float32)
        + lax.dot_general(norm_hi, w_lo, contract, preferred_element_type=jnp.float32)
        + lax.dot_general(norm_lo, w_hi, contract, preferred_element_type=jnp.float32)
    )
    count, share, block = o_ref.shape[0], 64, o_ref.shape[2]
    share = block // count
    chunk = 128
    band = chunk + lags
    span = block + chunk
    for m in range(block // chunk):
        low = depth - band - chunk * m
        rows_at = slice(chunk * m, chunk * (m + 1))
        cols_at = slice(low, low + band)
        out_at = slice(low, low + span)
        left = jnp.concatenate([w_hi[rows_at, cols_at], w_hi[rows_at, cols_at], w_lo[rows_at, cols_at]], axis=1)
        right = jnp.concatenate([skew_hi[cols_at, out_at], skew_lo[cols_at, out_at], skew_hi[cols_at, out_at]], axis=0)
        part = jnp.dot(left, right, preferred_element_type=jnp.float32)
        lined = pltpu.roll(part, span - (chunk - 1), 1, stride=1, stride_axis=0)
        for h in range(chunk // share):
            o_ref[(chunk * m) // share + h, 0:share, :] = lined[share * h : share * (h + 1), :block]
    extra = o_ref.shape[1] - share
    tail_rows = jnp.concatenate(
        [csum_ref[...], row_sum[0:1, :], jnp.zeros((extra - 2, block), jnp.float32)], axis=0
    )
    for k in range(count):
        o_ref[k, share:, :] = tail_rows


def lag_total(row_rev, col_pad, col_norm, col_sum, weights, count, lags):
    depth = weights.shape[1]
    width = col_pad.shape[0]
    block = weights.shape[0]
    share = block // count
    flops = 2 * depth * width * col_pad.shape[1] + 6 * 2 * block * (128 + lags) * (block + 128)
    return pl.pallas_call(
        functools.partial(lag_kernel, lags),
        out_shape=jax.ShapeDtypeStruct((count, share + 8, block), jnp.float32),
        in_specs=[pl.BlockSpec(memory_space=pltpu.VMEM)] * 5,
        out_specs=pl.BlockSpec(memory_space=pltpu.VMEM),
        cost_estimate=pl.CostEstimate(
            flops=flops, transcendentals=0, bytes_accessed=4 * (block * block + block * depth) + 2 * (depth + width) * 256
        ),
    )(row_rev, col_pad, col_norm, col_sum, weights)


def shards(snapshots, offsets, window_len, cone_exp):
    block = snapshots.shape[0]
    lags = LAGS
    history = shifted(snapshots, "col", 1)[block - lags :]
    col_ext = jnp.concatenate([history, snapshots], axis=0)
    chosen = pick(offsets, lax.axis_index("row"))
    pieces = broadcast_block(snapshots, chosen)
    me = lax.axis_index("col")
    extent = block + lags
    lengths = window_len.reshape(-1, block)
    exps = cone_exp.reshape(-1, block)
    row_weights = reversed_cone(pick(lengths, chosen), pick(exps, chosen), lags, extent)
    col_weights = cone_matrix(pick(lengths, me), pick(exps, me), lags + 1)
    col_wide = col_ext.astype(jnp.float32)
    col_part = jnp.sum(col_wide * col_wide, axis=1)
    col_sum = jnp.sum(col_weights * col_part[None, :], axis=1)
    n_chan = lax.axis_size("chan")
    share = block // n_chan
    payload = lag_total(pieces, col_ext, col_part[None, :], col_sum[None, :], row_weights, n_chan, lags)
    mine = jnp.sum(lax.all_to_all(payload, "chan", 0, 0, tiled=False), axis=0)
    row_sum = lax.dynamic_slice_in_dim(mine[share + 1], lax.axis_index("chan") * share, share)
    row_scale = jnp.sqrt(row_sum / C + epsilon)
    col_scale = jnp.sqrt(mine[share] / C + epsilon)
    return jnp.exp(-mine[:share] / (2.0 * C * row_scale[:, None] * col_scale[None, :]))


def solution(mesh):
    in_specs = (P("col", "chan"), P(), P(), P())
    out_specs = P(("row", "chan"), "col")
    return jax.shard_map(shards, mesh=mesh, in_specs=in_specs, out_specs=out_specs, check_vma=False)
```
